256 devices in a mesh: row: 8 (over y_lo, x), col: 32 (over y_hi, z, core).
Axes of the slice: x: 4, y: 4 (y_hi: 2, y_lo: 2; y = y_hi * 2 + y_lo), z: 8, core: 2. Of those that a mesh axis runs over, the one named last changes fastest.
Arguments:
- features: bfloat16 [65536, 256], P(('col', 'row')), may hold values from -6 to 6
- weight: bfloat16 [256, 256], replicated, may hold values from -0.375 to 0.375
- cotangent: bfloat16 [65536, 256], P(('row', 'col')), may hold values from -6 to 6
- tile_rows: int32 [8, 32, 176], P('row', 'col'), may hold values from 0 to 63
- tile_cols: int32 [8, 32, 176], P('row', 'col'), may hold values from 0 to 15
- tile_weights: int32 [8, 32, 176, 128, 128], P('row', 'col'), may hold values from 0 to 3, as said below
- tile_count: int32 [8, 32], P('row', 'col'), may hold values from 44 to 176, as said below
Outputs:
- hidden: bfloat16 [65536, 256], P(('row', 'col'))
- weight_grad: float32 [256, 256], replicated
- feature_grad: bfloat16 [65536, 256], P(('col', 'row'))
The draws below stay inside these ranges and needn't reach their ends.
Inputs may be any that keep to these rules, and one draw needn't show every extreme that they name: `tile_count`: one row group and column group has all 176 slots live, another a quarter of them. `tile_weights`: about one entry in 128 is nonzero.
All inputs are finite; a program needn't handle non-finite values.
Results may differ from the reference program's by a relative error of at most 0.006.
Values may be sent and summed in bfloat16 or wider, within the bound.
No kernel may reach another device: no remote copies, remote signals or barrier semaphores. Data moves between devices by JAX's collectives and lax.ppermute only.
A program may use at most 128 MiB of HBM per device.

```python
import math
import jax
import jax.numpy as jnp
from jax import lax

F = 256
TILE = 128
SPARSITY = 128
NODE_DEV = 256
RB = 64
CB = 16
SLOTS = 176
FAN = 88
NODES = 65536
N_ROW = 8
N_COL = 32


def draw_tile_weights(key, part):
    key_a = jax.random.fold_in(key, 21)
    key_b = jax.random.fold_in(key, 22)
    shape = (N_ROW, N_COL, SLOTS, TILE, TILE)
    present = jax.random.randint(key_a, shape, 0, SPARSITY) == 0
    values = jax.random.randint(key_b, shape, 1, 4)
    return jnp.where(present, values, 0).astype(jnp.int32)


def draw_tile_count(key, part):
    total = N_ROW * N_COL
    key_a = jax.random.fold_in(key, 11)
    key_b = jax.random.fold_in(key, 12)
    key_c = jax.random.fold_in(key, 13)
    key_d = jax.random.fold_in(key, 14)
    counts = jax.random.randint(key_a, (total,), SLOTS // 4, SLOTS // 2 + 1)
    busy = jax.random.randint(key_d, (total,), 0, 16) == 0
    counts = jnp.where(busy, SLOTS, counts)
    first = jax.random.randint(key_b, (), 0, total)
    second = (first + 1 + jax.random.randint(key_c, (), 0, total - 1)) % total
    places = jnp.arange(total)
    counts = jnp.where(places == first, SLOTS, jnp.where(places == second, SLOTS // 4, counts))
    return counts.astype(jnp.int32).reshape(N_ROW, N_COL)


def plant(values, key, smallest, high):
    index_at = [jax.random.randint(jax.random.fold_in(key, axis), (), 0, length) for axis, length in enumerate(values.shape)]
    longest = values.shape.index(max(values.shape))
    next_to = index_at[:longest] + [(index_at[longest] + 1) % values.shape[longest]] + index_at[longest + 1:]
    return values.at[tuple(index_at)].set(smallest).at[tuple(next_to)].set(high)


def levels(key, extent, cuts, least, top_value):
    gain, own = 1.0, jax.random.fold_in(key, 6)
    for position, parts in cuts:
        draws = jnp.exp(jax.random.uniform(jax.random.fold_in(own, position), (parts,), jnp.float32, least / len(cuts), top_value / len(cuts)))
        gain = gain * jnp.repeat(draws, extent[position] // parts).reshape([-1 if axis == position else 1 for axis in range(len(extent))])
    return gain


def bell_draw(rng, shape, scale, limit, shards=(), kind=jnp.bfloat16):
    array = jax.random.normal(rng, shape, jnp.float32) * scale
    if len(shards) > 0:
        array = levels(rng, shape, shards, -0.22, 0.18) * array
    return jnp.clip(array, min=-limit, max=limit).astype(kind)


def setup_inputs(seed: int = 0) -> dict:
    splits = jax.random.split(jax.random.key(seed), 8)
    return {
        "features": bell_draw(splits[0], (NODES, F), 1.0, 6.0, ((0, 256),)),
        "weight": bell_draw(splits[1], (F, F), F ** -0.5, 0.375),
        "cotangent": bell_draw(splits[2], (NODES, F), 1.0, 6.0, ((0, 256),)),
        "tile_rows": plant(jax.random.randint(splits[3], (N_ROW, N_COL, SLOTS), 0, RB), jax.random.fold_in(splits[3], 1), 0, RB - 1).astype(jnp.int32),
        "tile_cols": plant(jax.random.randint(splits[4], (N_ROW, N_COL, SLOTS), 0, CB), jax.random.fold_in(splits[4], 1), 0, CB - 1).astype(jnp.int32),
        "tile_weights": draw_tile_weights(jax.random.fold_in(splits[7], 71), 0),
        "tile_count": draw_tile_count(jax.random.fold_in(splits[7], 71), 0),
    }


def reference(features, weight, cotangent, tile_rows, tile_cols, tile_weights, tile_count):
    scale = 1.0 / math.sqrt(2.0 * FAN)
    row_len = NODE_DEV * N_COL
    col_len = NODE_DEV * N_ROW
    row_tiles = row_len // TILE
    col_tiles = col_len // TILE
    feats = features.astype(jnp.float32)
    slot_index = jnp.arange(SLOTS, dtype=jnp.int32)

    def block_terms(device):
        group_r = (device // N_COL).astype(jnp.int32)
        group_c = (device % N_COL).astype(jnp.int32)
        live = tile_count[group_r, group_c]
        alive = (slot_index < live).astype(jnp.float32)
        tiles = tile_weights[group_r, group_c].astype(jnp.float32) * alive[:, None, None]
        return (group_r, group_c, tiles, tile_rows[group_r, group_c], tile_cols[group_r, group_c])

    def forward_device(carry, device):
        group_r, group_c, tiles, row_ids, col_ids = block_terms(device)
        source = lax.dynamic_slice_in_dim(feats, (group_c * col_len).astype(jnp.int32), col_len, 0)
        pieces = source.reshape(col_tiles, TILE, F)[col_ids]
        products = jnp.einsum('sij,sjf->sif', tiles, pieces, precision=lax.Precision.HIGHEST)
        summed = jax.ops.segment_sum(products, row_ids, num_segments=row_tiles).reshape(row_len, F)
        start = (group_r * row_len).astype(jnp.int32)
        current = lax.dynamic_slice_in_dim(carry, start, row_len, 0)
        return (lax.dynamic_update_slice_in_dim(carry, current + summed, start, 0), None)
    devices = jnp.arange(N_ROW * N_COL, dtype=jnp.int32)
    total, unused = lax.scan(forward_device, jnp.zeros((NODES, F), jnp.float32), devices)
    aggregate = (total * scale).astype(jnp.bfloat16)
    preact = jnp.dot(aggregate, weight, preferred_element_type=jnp.float32)
    hidden = jax.nn.silu(preact).astype(jnp.bfloat16)
    sigma = jax.nn.sigmoid(preact)
    grad_pre = (cotangent.astype(jnp.float32) * sigma * (1.0 + preact * (1.0 - sigma))).astype(jnp.bfloat16)
    weight_grad = jnp.dot(aggregate.T, grad_pre, preferred_element_type=jnp.float32) / math.sqrt(NODES)
    grad_agg = jnp.dot(grad_pre, weight.T, preferred_element_type=jnp.float32).astype(jnp.bfloat16)
    grads = grad_agg.astype(jnp.float32)

    def backward_device(carry, device):
        group_r, group_c, tiles, row_ids, col_ids = block_terms(device)
        source = lax.dynamic_slice_in_dim(grads, (group_r * row_len).astype(jnp.int32), row_len, 0)
        pieces = source.reshape(row_tiles, TILE, F)[row_ids]
        products = jnp.einsum('sji,sjf->sif', tiles, pieces, precision=lax.Precision.HIGHEST)
        summed = jax.ops.segment_sum(products, col_ids, num_segments=col_tiles).reshape(col_len, F)
        start = (group_c * col_len).astype(jnp.int32)
        current = lax.dynamic_slice_in_dim(carry, start, col_len, 0)
        return (lax.dynamic_update_slice_in_dim(carry, current + summed, start, 0), None)
    back_total, unused2 = lax.scan(backward_device, jnp.zeros((NODES, F), jnp.float32), devices)
    feature_grad = (back_total * scale).astype(jnp.bfloat16)
    return (hidden, weight_grad, feature_grad)
```

```python
import functools
import math

import jax
import jax.numpy as jnp
from jax import lax
from jax.experimental import pallas as pl
from jax.experimental.pallas import tpu as pltpu
from jax.sharding import PartitionSpec as P

SPARSITY = 128


def slot_kernel(live_ref, rows_ref, cols_ref, tiles_ref, src_ref, out_ref, *, per_block, scale, transpose):
    block_id = pl.program_id(0)

    @pl.when(block_id == 0)
    def _():
        out_ref[...] = jnp.zeros_like(out_ref)

    live = live_ref[0]
    for k in range(per_block):
        slot = block_id * per_block + k

        @pl.when(slot < live)
        def _():
            tile_vals = tiles_ref[k].astype(jnp.bfloat16)
            if transpose:
                piece = src_ref[rows_ref[slot]]
                product = lax.dot_general(
                    tile_vals, piece, (((0,), (0,)), ((), ())), preferred_element_type=jnp.float32
                )
                target = cols_ref[slot]
            else:
                piece = src_ref[cols_ref[slot]]
                product = jnp.dot(tile_vals, piece, preferred_element_type=jnp.float32)
                target = rows_ref[slot]
            out_ref[target] += product

    @pl.when(block_id == pl.num_programs(0) - 1)
    def _():
        out_ref[...] = out_ref[...] * scale


def slot_pass(live, row_ids, col_ids, tiles, source_tiles, out_tiles, scale, transpose):
    slot_total, tile_len, _ = tiles.shape
    width = source_tiles.shape[-1]
    per_block = math.gcd(slot_total, 16)

    def tile_block(block_id, live_ref, rows_ref, cols_ref):
        last = jnp.maximum(live_ref[0] - 1, 0) // per_block
        return (jnp.minimum(block_id, last), 0, 0)

    def whole(block_id, live_ref, rows_ref, cols_ref):
        return (0, 0, 0)

    grid_spec = pltpu.PrefetchScalarGridSpec(
        num_scalar_prefetch=3,
        grid=(slot_total // per_block,),
        in_specs=[
            pl.BlockSpec((per_block, tile_len, tile_len), tile_block),
            pl.BlockSpec(source_tiles.shape, whole),
        ],
        out_specs=pl.BlockSpec((out_tiles, tile_len, width), whole),
    )
    return pl.pallas_call(
        functools.partial(slot_kernel, per_block=per_block, scale=scale, transpose=transpose),
        grid_spec=grid_spec,
        out_shape=jax.ShapeDtypeStruct((out_tiles, tile_len, width), jnp.float32),
        compiler_params=pltpu.CompilerParams(
            dimension_semantics=("arbitrary",), vmem_limit_bytes=48 * 1024 * 1024
        ),
    )(live, row_ids, col_ids, tiles, source_tiles)


def dense_layer(aggregate, weight, cotangent):
    preact = jnp.dot(aggregate, weight, preferred_element_type=jnp.float32)
    hidden = jax.nn.silu(preact).astype(jnp.bfloat16)
    sigma = jax.nn.sigmoid(preact)
    grad_pre = (cotangent.astype(jnp.float32) * sigma * (1.0 + preact * (1.0 - sigma))).astype(
        jnp.bfloat16
    )
    return (hidden, grad_pre)


def on_device(features, weight, cotangent, tile_rows, tile_cols, tile_weights, tile_count):
    node_dev = cotangent.shape[0]
    width = features.shape[1]
    slot_total = tile_weights.shape[2]
    tile_len = tile_weights.shape[-1]
    sparsity_value = SPARSITY
    fan_value = slot_total * tile_len * tile_len // (node_dev * sparsity_value)
    scale = 1.0 / math.sqrt(2.0 * fan_value)
    row_len = node_dev * lax.axis_size("col")
    col_len = node_dev * lax.axis_size("row")
    row_tiles = row_len // tile_len
    col_tiles = col_len // tile_len
    nodes_all = row_len * lax.axis_size("row")
    row_ids = tile_rows[0, 0]
    col_ids = tile_cols[0, 0]
    weights_all = tile_weights[0, 0]
    live = tile_count[0, 0].reshape(1)
    source = lax.all_gather(features, "row", axis=0, tiled=True)
    source_tiles = source.reshape(col_tiles, tile_len, width)
    summed = slot_pass(live, row_ids, col_ids, weights_all, source_tiles, row_tiles, scale, False)
    partial_value = summed.reshape(row_len, width)
    aggregate = lax.psum_scatter(partial_value, "col", scatter_dimension=0, tiled=True).astype(
        jnp.bfloat16
    )
    hidden, grad_own = dense_layer(aggregate, weight, cotangent)
    weight_part = lax.dot_general(
        aggregate, grad_own, (((0,), (0,)), ((), ())), preferred_element_type=jnp.float32
    )
    grad_agg = jnp.dot(grad_own, weight.T, preferred_element_type=jnp.float32).astype(jnp.bfloat16)
    weight_grad = lax.psum(weight_part, ("row", "col")) / math.sqrt(nodes_all)
    grad_source = lax.all_gather(grad_agg, "col", axis=0, tiled=True)
    grad_tiles = grad_source.reshape(row_tiles, tile_len, width)
    back_summed = slot_pass(live, row_ids, col_ids, weights_all, grad_tiles, col_tiles, scale, True)
    back_partial = back_summed.reshape(col_len, width)
    feature_grad = lax.psum_scatter(back_partial, "row", scatter_dimension=0, tiled=True).astype(
        jnp.bfloat16
    )
    return (hidden, weight_grad, feature_grad)


def solution(mesh):
    in_specs = (
        P(("col", "row"), None),
        P(),
        P(("row", "col"), None),
        P("row", "col", None),
        P("row", "col", None),
        P("row", "col", None, None, None),
        P("row", "col"),
    )
    out_specs = (P(("row", "col"), None), P(), P(("col", "row"), None))
    return jax.shard_map(
        on_device, mesh=mesh, in_specs=in_specs, out_specs=out_specs, check_vma=False
    )
```

```python
import functools
import math

import jax
import jax.numpy as jnp
from jax import lax
from jax.experimental import pallas as pl
from jax.experimental.pallas import tpu as pltpu
from jax.sharding import Mesh
from jax.sharding import PartitionSpec as P

SPARSITY = 128


def slot_kernel(live_ref, rows_ref, cols_ref, tiles_ref, src_ref, out_ref, *, per_block, scale, transpose):
    block_id = pl.program_id(0)

    @pl.when(block_id == 0)
    def _():
        out_ref[...] = jnp.zeros_like(out_ref)

    live = live_ref[0]
    for k in range(per_block):
        slot = block_id * per_block + k

        @pl.when(slot < live)
        def _():
            tile_vals = tiles_ref[k].astype(jnp.bfloat16)
            if transpose:
                piece = src_ref[rows_ref[slot]]
                product = lax.dot_general(
                    tile_vals, piece, (((0,), (0,)), ((), ())), preferred_element_type=jnp.float32
                )
                target = cols_ref[slot]
            else:
                piece = src_ref[cols_ref[slot]]
                product = jnp.dot(tile_vals, piece, preferred_element_type=jnp.float32)
                target = rows_ref[slot]
            out_ref[target] += product

    @pl.when(block_id == pl.num_programs(0) - 1)
    def _():
        out_ref[...] = out_ref[...] * scale


def slot_pass(live, row_ids, col_ids, tiles, source_tiles, out_tiles, scale, transpose):
    slot_total, tile_len, _ = tiles.shape
    width = source_tiles.shape[-1]
    per_block = math.gcd(slot_total, 16)

    def tile_block(block_id, live_ref, rows_ref, cols_ref):
        last = jnp.maximum(live_ref[0] - 1, 0) // per_block
        return (jnp.minimum(block_id, last), 0, 0)

    def whole(block_id, live_ref, rows_ref, cols_ref):
        return (0, 0, 0)

    grid_spec = pltpu.PrefetchScalarGridSpec(
        num_scalar_prefetch=3,
        grid=(slot_total // per_block,),
        in_specs=[
            pl.BlockSpec((per_block, tile_len, tile_len), tile_block),
            pl.BlockSpec(source_tiles.shape, whole),
        ],
        out_specs=pl.BlockSpec((out_tiles, tile_len, width), whole),
    )
    return pl.pallas_call(
        functools.partial(slot_kernel, per_block=per_block, scale=scale, transpose=transpose),
        grid_spec=grid_spec,
        out_shape=jax.ShapeDtypeStruct((out_tiles, tile_len, width), jnp.float32),
        compiler_params=pltpu.CompilerParams(
            dimension_semantics=("arbitrary",), vmem_limit_bytes=48 * 1024 * 1024
        ),
    )(live, row_ids, col_ids, tiles, source_tiles)


def dense_layer(aggregate, weight, cotangent):
    preact = jnp.dot(aggregate, weight, preferred_element_type=jnp.float32)
    hidden = jax.nn.silu(preact).astype(jnp.bfloat16)
    sigma = jax.nn.sigmoid(preact)
    grad_pre = (cotangent.astype(jnp.float32) * sigma * (1.0 + preact * (1.0 - sigma))).astype(
        jnp.bfloat16
    )
    return (hidden, grad_pre)


def butterfly_sum(value, axes, count):
    for level in reversed(range(count.bit_length() - 1)):
        pairs = [(i, i ^ (1 << level)) for i in range(count)]
        value = value + lax.ppermute(value, axes, pairs)
    return value


def on_device(
    features, weight, cotangent, tile_rows, tile_cols, tile_weights, tile_count, *, sizes
):
    row_n, high_n, mid_n, core_n = sizes
    col_axes = ("high", "mid", "core")
    col_n = high_n * mid_n * core_n
    node_dev = cotangent.shape[0]
    width = features.shape[1]
    slot_total = tile_weights.shape[2]
    tile_len = tile_weights.shape[-1]
    sparsity_value = SPARSITY
    fan_value = slot_total * tile_len * tile_len // (node_dev * sparsity_value)
    scale = 1.0 / math.sqrt(2.0 * fan_value)
    row_len = node_dev * col_n
    col_len = node_dev * row_n
    row_tiles = row_len // tile_len
    col_tiles = col_len // tile_len
    nodes_all = row_len * row_n
    per_chunk = node_dev // tile_len
    row_ids = tile_rows[0, 0]
    col_ids = tile_cols[0, 0]
    chunk = row_ids // per_chunk
    high_i = chunk // (mid_n * core_n)
    mid_i = (chunk // core_n) % mid_n
    core_i = chunk % core_n
    placed = (core_i * mid_n * high_n + mid_i * high_n + high_i) * per_chunk + row_ids % per_chunk
    weights_all = tile_weights[0, 0]
    live = tile_count[0, 0].reshape(1)
    source = lax.all_gather(features, "row", axis=0, tiled=True)
    source_tiles = source.reshape(col_tiles, tile_len, width)
    summed = slot_pass(live, placed, col_ids, weights_all, source_tiles, row_tiles, scale, False)
    partial_value = summed.reshape(row_len, width)
    partial_value = lax.psum_scatter(partial_value, "core", scatter_dimension=0, tiled=True)
    partial_value = lax.psum_scatter(partial_value, "mid", scatter_dimension=0, tiled=True)
    partial_value = lax.psum_scatter(partial_value, "high", scatter_dimension=0, tiled=True)
    aggregate = partial_value.astype(jnp.bfloat16)
    hidden, grad_own = dense_layer(aggregate, weight, cotangent)
    weight_part = lax.dot_general(
        aggregate, grad_own, (((0,), (0,)), ((), ())), preferred_element_type=jnp.float32
    )
    grad_agg = jnp.dot(grad_own, weight.T, preferred_element_type=jnp.float32).astype(jnp.bfloat16)
    weight_sum = butterfly_sum(weight_part, ("row",) + col_axes, row_n * col_n)
    weight_grad = weight_sum / math.sqrt(nodes_all)
    grad_source = lax.all_gather(grad_agg, "high", axis=0, tiled=True)
    grad_source = lax.all_gather(grad_source, "mid", axis=0, tiled=True)
    grad_source = lax.all_gather(grad_source, "core", axis=0, tiled=True)
    grad_tiles = grad_source.reshape(row_tiles, tile_len, width)
    back_summed = slot_pass(live, placed, col_ids, weights_all, grad_tiles, col_tiles, scale, True)
    back_partial = back_summed.reshape(col_len, width)
    feature_grad = lax.psum_scatter(back_partial, "row", scatter_dimension=0, tiled=True).astype(
        jnp.bfloat16
    )
    return (hidden, weight_grad, feature_grad)


def solution(mesh):
    row_n, col_n = mesh.shape["row"], mesh.shape["col"]
    core_n = 2
    high_n = 2
    mid_n = col_n // (high_n * core_n)
    sizes = (row_n, high_n, mid_n, core_n)
    fine = Mesh(mesh.devices.reshape(sizes), ("row", "high", "mid", "core"))
    col = ("high", "mid", "core")
    in_specs = (
        P(col + ("row",), None),
        P(),
        P(("row",) + col, None),
        P("row", col, None),
        P("row", col, None),
        P("row", col, None, None, None),
        P("row", col),
    )
    out_specs = (P(("row",) + col, None), P(), P(col + ("row",), None))
    return jax.shard_map(
        functools.partial(on_device, sizes=sizes),
        mesh=fine,
        in_specs=in_specs,
        out_specs=out_specs,
        check_vma=False,
    )
```

```python
import functools
import math

import jax
import jax.numpy as jnp
from jax import lax
from jax.experimental import pallas as pl
from jax.experimental.pallas import tpu as pltpu
from jax.sharding import Mesh
from jax.sharding import PartitionSpec as P

SPARSITY = 128


def slot_kernel(live_ref, rows_ref, cols_ref, tiles_ref, src_ref, out_ref, *, per_block, scale, transpose):
    block_id = pl.program_id(0)

    @pl.when(block_id == 0)
    def _():
        out_ref[...] = jnp.zeros_like(out_ref)

    live = live_ref[0]
    for k in range(per_block):
        slot = block_id * per_block + k

        @pl.when(slot < live)
        def _():
            tile_vals = tiles_ref[k].astype(jnp.bfloat16)
            if transpose:
                piece = src_ref[rows_ref[slot]]
                product = lax.dot_general(
                    tile_vals, piece, (((0,), (0,)), ((), ())), preferred_element_type=jnp.float32
                )
                target = cols_ref[slot]
            else:
                piece = src_ref[cols_ref[slot]]
                product = jnp.dot(tile_vals, piece, preferred_element_type=jnp.float32)
                target = rows_ref[slot]
            out_ref[target] += product

    @pl.when(block_id == pl.num_programs(0) - 1)
    def _():
        out_ref[...] = out_ref[...] * scale


def slot_pass(live, row_ids, col_ids, tiles, source_tiles, out_tiles, scale, transpose):
    slot_total, tile_len, _ = tiles.shape
    width = source_tiles.shape[-1]
    per_block = math.gcd(slot_total, 16)

    def tile_block(block_id, live_ref, rows_ref, cols_ref):
        last = jnp.maximum(live_ref[0] - 1, 0) // per_block
        return (jnp.minimum(block_id, last), 0, 0)

    def whole(block_id, live_ref, rows_ref, cols_ref):
        return (0, 0, 0)

    grid_spec = pltpu.PrefetchScalarGridSpec(
        num_scalar_prefetch=3,
        grid=(slot_total // per_block,),
        in_specs=[
            pl.BlockSpec((per_block, tile_len, tile_len), tile_block),
            pl.BlockSpec(source_tiles.shape, whole),
        ],
        out_specs=pl.BlockSpec((out_tiles, tile_len, width), whole),
    )
    return pl.pallas_call(
        functools.partial(slot_kernel, per_block=per_block, scale=scale, transpose=transpose),
        grid_spec=grid_spec,
        out_shape=jax.ShapeDtypeStruct((out_tiles, tile_len, width), jnp.float32),
        compiler_params=pltpu.CompilerParams(
            dimension_semantics=("arbitrary",), vmem_limit_bytes=48 * 1024 * 1024
        ),
    )(live, row_ids, col_ids, tiles, source_tiles)


def dense_layer(aggregate, weight, cotangent):
    preact = jnp.dot(aggregate, weight, preferred_element_type=jnp.float32)
    hidden = jax.nn.silu(preact).astype(jnp.bfloat16)
    sigma = jax.nn.sigmoid(preact)
    grad_pre = (cotangent.astype(jnp.float32) * sigma * (1.0 + preact * (1.0 - sigma))).astype(
        jnp.bfloat16
    )
    return (hidden, grad_pre)


def butterfly_sum(value, axes, count):
    for level in reversed(range(count.bit_length() - 1)):
        pairs = [(i, i ^ (1 << level)) for i in range(count)]
        value = value + lax.ppermute(value, axes, pairs)
    return value


def pair_scatter(value, axis):
    half = value.shape[0] // 2
    own = lax.axis_index(axis)
    keep = lax.dynamic_slice_in_dim(value, own * half, half, 0)
    send = lax.dynamic_slice_in_dim(value, (1 - own) * half, half, 0)
    return keep + lax.ppermute(send, axis, [(0, 1), (1, 0)])


def pair_gather(value, axis):
    own = lax.axis_index(axis)
    other = lax.ppermute(value, axis, [(0, 1), (1, 0)])
    first = jnp.where(own == 0, value, other)
    second = jnp.where(own == 0, other, value)
    return jnp.concatenate([first, second], axis=0)


def on_device(
    features, weight, cotangent, tile_rows, tile_cols, tile_weights, tile_count, *, sizes
):
    row_n, high_n, mid_n, core_n = sizes
    col_axes = ("high", "mid", "core")
    col_n = high_n * mid_n * core_n
    node_dev = cotangent.shape[0]
    width = features.shape[1]
    slot_total = tile_weights.shape[2]
    tile_len = tile_weights.shape[-1]
    sparsity_value = SPARSITY
    fan_value = slot_total * tile_len * tile_len // (node_dev * sparsity_value)
    scale = 1.0 / math.sqrt(2.0 * fan_value)
    row_len = node_dev * col_n
    col_len = node_dev * row_n
    row_tiles = row_len // tile_len
    col_tiles = col_len // tile_len
    nodes_all = row_len * row_n
    per_chunk = node_dev // tile_len
    row_ids = tile_rows[0, 0]
    col_ids = tile_cols[0, 0]
    chunk = row_ids // per_chunk
    high_i = chunk // (mid_n * core_n)
    mid_i = (chunk // core_n) % mid_n
    core_i = chunk % core_n
    placed = (core_i * mid_n * high_n + mid_i * high_n + high_i) * per_chunk + row_ids % per_chunk
    weights_all = tile_weights[0, 0]
    live = tile_count[0, 0].reshape(1)
    source = lax.all_gather(features, "row", axis=0, tiled=True)
    source_tiles = source.reshape(col_tiles, tile_len, width)
    summed = slot_pass(live, placed, col_ids, weights_all, source_tiles, row_tiles, scale, False)
    partial_value = summed.reshape(row_len, width)
    partial_value = pair_scatter(partial_value, "core")
    partial_value = lax.psum_scatter(partial_value, "mid", scatter_dimension=0, tiled=True)
    partial_value = pair_scatter(partial_value, "high")
    aggregate = partial_value.astype(jnp.bfloat16)
    hidden, grad_own = dense_layer(aggregate, weight, cotangent)
    weight_part = lax.dot_general(
        aggregate, grad_own, (((0,), (0,)), ((), ())), preferred_element_type=jnp.float32
    )
    grad_agg = jnp.dot(grad_own, weight.T, preferred_element_type=jnp.float32).astype(jnp.bfloat16)
    weight_sum = butterfly_sum(weight_part, ("row",) + col_axes, row_n * col_n)
    weight_grad = weight_sum / math.sqrt(nodes_all)
    grad_source = pair_gather(grad_agg, "high")
    grad_source = lax.all_gather(grad_source, "mid", axis=0, tiled=True)
    grad_source = pair_gather(grad_source, "core")
    grad_tiles = grad_source.reshape(row_tiles, tile_len, width)
    back_summed = slot_pass(live, placed, col_ids, weights_all, grad_tiles, col_tiles, scale, True)
    back_partial = back_summed.reshape(col_len, width)
    feature_grad = lax.psum_scatter(back_partial, "row", scatter_dimension=0, tiled=True).astype(
        jnp.bfloat16
    )
    return (hidden, weight_grad, feature_grad)


def solution(mesh):
    row_n, col_n = mesh.shape["row"], mesh.shape["col"]
    core_n = 2
    high_n = 2
    mid_n = col_n // (high_n * core_n)
    sizes = (row_n, high_n, mid_n, core_n)
    fine = Mesh(mesh.devices.reshape(sizes), ("row", "high", "mid", "core"))
    col = ("high", "mid", "core")
    in_specs = (
        P(col + ("row",), None),
        P(),
        P(("row",) + col, None),
        P("row", col, None),
        P("row", col, None),
        P("row", col, None, None, None),
        P("row", col),
    )
    out_specs = (P(("row",) + col, None), P(), P(col + ("row",), None))
    return jax.shard_map(
        functools.partial(on_device, sizes=sizes),
        mesh=fine,
        in_specs=in_specs,
        out_specs=out_specs,
        check_vma=False,
    )
```

```python
import functools
import math

import jax
import jax.numpy as jnp
from jax import lax
from jax.experimental import pallas as pl
from jax.experimental.pallas import tpu as pltpu
from jax.sharding import Mesh
from jax.sharding import PartitionSpec as P

SPARSITY = 128


def slot_kernel(live_ref, rows_ref, cols_ref, tiles_ref, src_ref, out_ref, *, per_block, scale, transpose):
    block_id = pl.program_id(0)

    @pl.when(block_id == 0)
    def _():
        out_ref[...] = jnp.zeros_like(out_ref)

    live = live_ref[0]
    for k in range(per_block):
        slot = block_id * per_block + k

        @pl.when(slot < live)
        def _():
            tile_vals = tiles_ref[k].astype(jnp.bfloat16)
            if transpose:
                piece = src_ref[rows_ref[slot]]
                product = lax.dot_general(
                    tile_vals, piece, (((0,), (0,)), ((), ())), preferred_element_type=jnp.float32
                )
                target = cols_ref[slot]
            else:
                piece = src_ref[cols_ref[slot]]
                product = jnp.dot(tile_vals, piece, preferred_element_type=jnp.float32)
                target = rows_ref[slot]
            out_ref[target] += product

    @pl.when(block_id == pl.num_programs(0) - 1)
    def _():
        out_ref[...] = out_ref[...] * scale


def slot_pass(live, row_ids, col_ids, tiles, source_tiles, out_tiles, scale, transpose):
    slot_total, tile_len, _ = tiles.shape
    width = source_tiles.shape[-1]
    per_block = math.gcd(slot_total, 16)

    def tile_block(block_id, live_ref, rows_ref, cols_ref):
        last = jnp.maximum(live_ref[0] - 1, 0) // per_block
        return (jnp.minimum(block_id, last), 0, 0)

    def whole(block_id, live_ref, rows_ref, cols_ref):
        return (0, 0, 0)

    grid_spec = pltpu.PrefetchScalarGridSpec(
        num_scalar_prefetch=3,
        grid=(slot_total // per_block,),
        in_specs=[
            pl.BlockSpec((per_block, tile_len, tile_len), tile_block),
            pl.BlockSpec(source_tiles.shape, whole),
        ],
        out_specs=pl.BlockSpec((out_tiles, tile_len, width), whole),
    )
    return pl.pallas_call(
        functools.partial(slot_kernel, per_block=per_block, scale=scale, transpose=transpose),
        grid_spec=grid_spec,
        out_shape=jax.ShapeDtypeStruct((out_tiles, tile_len, width), jnp.float32),
        compiler_params=pltpu.CompilerParams(
            dimension_semantics=("arbitrary",), vmem_limit_bytes=48 * 1024 * 1024
        ),
    )(live, row_ids, col_ids, tiles, source_tiles)


def dense_layer(aggregate, weight, cotangent):
    preact = jnp.dot(aggregate, weight, preferred_element_type=jnp.float32)
    hidden = jax.nn.silu(preact).astype(jnp.bfloat16)
    sigma = jax.nn.sigmoid(preact)
    grad_pre = (cotangent.astype(jnp.float32) * sigma * (1.0 + preact * (1.0 - sigma))).astype(
        jnp.bfloat16
    )
    return (hidden, grad_pre)


def butterfly_sum(value, axes, count, levels):
    for level in levels:
        pairs = [(i, i ^ (1 << level)) for i in range(count)]
        value = value + lax.ppermute(value, axes, pairs)
    return value


def doubling_gather(value, axis, count):
    own = lax.axis_index(axis)
    for level in range(count.bit_length() - 1):
        pairs = [(i, i ^ (1 << level)) for i in range(count)]
        other = lax.ppermute(value, axis, pairs)
        low = ((own >> level) & 1) == 0
        value = jnp.concatenate(
            [jnp.where(low, value, other), jnp.where(low, other, value)], axis=0
        )
    return value


def pair_scatter(value, axis):
    half = value.shape[0] // 2
    own = lax.axis_index(axis)
    keep = lax.dynamic_slice_in_dim(value, own * half, half, 0)
    send = lax.dynamic_slice_in_dim(value, (1 - own) * half, half, 0)
    return keep + lax.ppermute(send, axis, [(0, 1), (1, 0)])


def pair_gather(value, axis):
    own = lax.axis_index(axis)
    other = lax.ppermute(value, axis, [(0, 1), (1, 0)])
    first = jnp.where(own == 0, value, other)
    second = jnp.where(own == 0, other, value)
    return jnp.concatenate([first, second], axis=0)


def on_device(
    features, weight, cotangent, tile_rows, tile_cols, tile_weights, tile_count, *, sizes
):
    row_n, high_n, mid_n, core_n = sizes
    col_axes = ("high", "mid", "core")
    col_n = high_n * mid_n * core_n
    node_dev = cotangent.shape[0]
    width = features.shape[1]
    slot_total = tile_weights.shape[2]
    tile_len = tile_weights.shape[-1]
    sparsity_value = SPARSITY
    fan_value = slot_total * tile_len * tile_len // (node_dev * sparsity_value)
    scale = 1.0 / math.sqrt(2.0 * fan_value)
    row_len = node_dev * col_n
    col_len = node_dev * row_n
    row_tiles = row_len // tile_len
    col_tiles = col_len // tile_len
    nodes_all = row_len * row_n
    per_chunk = node_dev // tile_len
    row_ids = tile_rows[0, 0]
    col_ids = tile_cols[0, 0]
    chunk = row_ids // per_chunk
    high_i = chunk // (mid_n * core_n)
    mid_i = (chunk // core_n) % mid_n
    core_i = chunk % core_n
    placed = (core_i * mid_n * high_n + mid_i * high_n + high_i) * per_chunk + row_ids % per_chunk
    weights_all = tile_weights[0, 0]
    live = tile_count[0, 0].reshape(1)
    source = doubling_gather(features, "row", row_n)
    source_tiles = source.reshape(col_tiles, tile_len, width)
    summed = slot_pass(live, placed, col_ids, weights_all, source_tiles, row_tiles, scale, False)
    partial_value = summed.reshape(row_len, width)
    partial_value = pair_scatter(partial_value, "core")
    partial_value = lax.psum_scatter(partial_value, "mid", scatter_dimension=0, tiled=True)
    partial_value = pair_scatter(partial_value, "high")
    aggregate = partial_value.astype(jnp.bfloat16)
    hidden, grad_own = dense_layer(aggregate, weight, cotangent)
    weight_part = lax.dot_general(
        aggregate, grad_own, (((0,), (0,)), ((), ())), preferred_element_type=jnp.float32
    )
    grad_agg = jnp.dot(grad_own, weight.T, preferred_element_type=jnp.float32).astype(jnp.bfloat16)
    every = ("row",) + col_axes
    levels = list(reversed(range((row_n * col_n).bit_length() - 1)))
    weight_sum = butterfly_sum(weight_part, every, row_n * col_n, levels)
    grad_source = pair_gather(grad_agg, "high")
    grad_source = lax.all_gather(grad_source, "mid", axis=0, tiled=True)
    grad_source = pair_gather(grad_source, "core")
    grad_tiles = grad_source.reshape(row_tiles, tile_len, width)
    back_summed = slot_pass(live, placed, col_ids, weights_all, grad_tiles, col_tiles, scale, True)
    back_partial = back_summed.reshape(col_len, width)
    feature_grad = lax.psum_scatter(back_partial, "row", scatter_dimension=0, tiled=True).astype(
        jnp.bfloat16
    )
    weight_grad = weight_sum / math.sqrt(nodes_all)
    return (hidden, weight_grad, feature_grad)


def solution(mesh):
    row_n, col_n = mesh.shape["row"], mesh.shape["col"]
    core_n = 2
    high_n = 2
    mid_n = col_n // (high_n * core_n)
    sizes = (row_n, high_n, mid_n, core_n)
    fine = Mesh(mesh.devices.reshape(sizes), ("row", "high", "mid", "core"))
    col = ("high", "mid", "core")
    in_specs = (
        P(col + ("row",), None),
        P(),
        P(("row",) + col, None),
        P("row", col, None),
        P("row", col, None),
        P("row", col, None, None, None),
        P("row", col),
    )
    out_specs = (P(("row",) + col, None), P(), P(col + ("row",), None))
    return jax.shard_map(
        functools.partial(on_device, sizes=sizes),
        mesh=fine,
        in_specs=in_specs,
        out_specs=out_specs,
        check_vma=False,
    )
```

```python
import functools
import math

import jax
import jax.numpy as jnp
from jax import lax
from jax.experimental import pallas as pl
from jax.experimental.pallas import tpu as pltpu
from jax.sharding import Mesh
from jax.sharding import PartitionSpec as P

SPARSITY = 128


def slot_kernel(live_ref, rows_ref, cols_ref, tiles_ref, src_ref, out_ref, *, per_block, scale, transpose):
    block_id = pl.program_id(0)

    @pl.when(block_id == 0)
    def _():
        out_ref[...] = jnp.zeros_like(out_ref)

    live = live_ref[0]
    for k in range(per_block):
        slot = block_id * per_block + k

        @pl.when(slot < live)
        def _():
            tile_vals = tiles_ref[k].astype(jnp.bfloat16)
            if transpose:
                piece = src_ref[rows_ref[slot]]
                product = lax.dot_general(
                    tile_vals, piece, (((0,), (0,)), ((), ())), preferred_element_type=jnp.float32
                )
                target = cols_ref[slot]
            else:
                piece = src_ref[cols_ref[slot]]
                product = jnp.dot(tile_vals, piece, preferred_element_type=jnp.float32)
                target = rows_ref[slot]
            out_ref[target] += product

    @pl.when(block_id == pl.num_programs(0) - 1)
    def _():
        out_ref[...] = out_ref[...] * scale


def slot_pass(live, row_ids, col_ids, tiles, source_tiles, out_tiles, scale, transpose):
    slot_total, tile_len, _ = tiles.shape
    width = source_tiles.shape[-1]
    per_block = math.gcd(slot_total, 16)

    def tile_block(block_id, live_ref, rows_ref, cols_ref):
        last = jnp.maximum(live_ref[0] - 1, 0) // per_block
        return (jnp.minimum(block_id, last), 0, 0)

    def whole(block_id, live_ref, rows_ref, cols_ref):
        return (0, 0, 0)

    grid_spec = pltpu.PrefetchScalarGridSpec(
        num_scalar_prefetch=3,
        grid=(slot_total // per_block,),
        in_specs=[
            pl.BlockSpec((per_block, tile_len, tile_len), tile_block),
            pl.BlockSpec(source_tiles.shape, whole),
        ],
        out_specs=pl.BlockSpec((out_tiles, tile_len, width), whole),
    )
    return pl.pallas_call(
        functools.partial(slot_kernel, per_block=per_block, scale=scale, transpose=transpose),
        grid_spec=grid_spec,
        out_shape=jax.ShapeDtypeStruct((out_tiles, tile_len, width), jnp.float32),
        compiler_params=pltpu.CompilerParams(
            dimension_semantics=("arbitrary",), vmem_limit_bytes=48 * 1024 * 1024
        ),
    )(live, row_ids, col_ids, tiles, source_tiles)


def dense_layer(aggregate, weight, cotangent):
    preact = jnp.dot(aggregate, weight, preferred_element_type=jnp.float32)
    hidden = jax.nn.silu(preact).astype(jnp.bfloat16)
    sigma = jax.nn.sigmoid(preact)
    grad_pre = (cotangent.astype(jnp.float32) * sigma * (1.0 + preact * (1.0 - sigma))).astype(
        jnp.bfloat16
    )
    return (hidden, grad_pre)


def butterfly_sum(value, axes, count, levels):
    for level in levels:
        pairs = [(i, i ^ (1 << level)) for i in range(count)]
        value = value + lax.ppermute(value, axes, pairs)
    return value


def doubling_gather(value, axis, count):
    own = lax.axis_index(axis)
    for level in range(count.bit_length() - 1):
        pairs = [(i, i ^ (1 << level)) for i in range(count)]
        other = lax.ppermute(value, axis, pairs)
        low = ((own >> level) & 1) == 0
        value = jnp.concatenate(
            [jnp.where(low, value, other), jnp.where(low, other, value)], axis=0
        )
    return value


def pair_scatter(value, axis):
    half = value.shape[0] // 2
    own = lax.axis_index(axis)
    keep = lax.dynamic_slice_in_dim(value, own * half, half, 0)
    send = lax.dynamic_slice_in_dim(value, (1 - own) * half, half, 0)
    return keep + lax.ppermute(send, axis, [(0, 1), (1, 0)])


def pair_gather(value, axis):
    own = lax.axis_index(axis)
    other = lax.ppermute(value, axis, [(0, 1), (1, 0)])
    first = jnp.where(own == 0, value, other)
    second = jnp.where(own == 0, other, value)
    return jnp.concatenate([first, second], axis=0)


def split_bf16(value):
    high = value.astype(jnp.bfloat16)
    low = (value - high.astype(jnp.float32)).astype(jnp.bfloat16)
    return high, low


def carried_gather(value, carried, axis, count):
    own = lax.axis_index(axis)
    rows = carried.shape[0]
    for level in range(count.bit_length() - 1):
        pairs = [(i, i ^ (1 << level)) for i in range(count)]
        high, low = split_bf16(carried)
        length = value.shape[0]
        packet = lax.ppermute(jnp.concatenate([value, high, low], axis=0), axis, pairs)
        other = packet[:length]
        other_high = packet[length : length + rows].astype(jnp.float32)
        other_low = packet[length + rows :].astype(jnp.float32)
        low_side = ((own >> level) & 1) == 0
        value = jnp.concatenate(
            [jnp.where(low_side, value, other), jnp.where(low_side, other, value)], axis=0
        )
        mine = high.astype(jnp.float32) + low.astype(jnp.float32)
        carried = mine + (other_high + other_low)
    return value, carried


def carried_scatter(value, carried, axis, count):
    own = lax.axis_index(axis)
    for level in reversed(range(count.bit_length() - 1)):
        pairs = [(i, i ^ (1 << level)) for i in range(count)]
        half = value.shape[0] // 2
        upper = (own >> level) & 1
        keep = lax.dynamic_slice_in_dim(value, upper * half, half, 0)
        send = lax.dynamic_slice_in_dim(value, (1 - upper) * half, half, 0)
        packet = lax.ppermute(jnp.concatenate([send, carried], axis=0), axis, pairs)
        value = keep + packet[:half]
        carried = carried + packet[half:]
    return value, carried


def on_device(
    features, weight, cotangent, tile_rows, tile_cols, tile_weights, tile_count, *, sizes
):
    row_n, high_n, mid_n, core_n = sizes
    col_axes = ("high", "mid", "core")
    col_n = high_n * mid_n * core_n
    node_dev = cotangent.shape[0]
    width = features.shape[1]
    slot_total = tile_weights.shape[2]
    tile_len = tile_weights.shape[-1]
    sparsity_value = SPARSITY
    fan_value = slot_total * tile_len * tile_len // (node_dev * sparsity_value)
    scale = 1.0 / math.sqrt(2.0 * fan_value)
    row_len = node_dev * col_n
    col_len = node_dev * row_n
    row_tiles = row_len // tile_len
    col_tiles = col_len // tile_len
    nodes_all = row_len * row_n
    per_chunk = node_dev // tile_len
    row_ids = tile_rows[0, 0]
    col_ids = tile_cols[0, 0]
    chunk = row_ids // per_chunk
    high_i = chunk // (mid_n * core_n)
    mid_i = (chunk // core_n) % mid_n
    core_i = chunk % core_n
    placed = (core_i * mid_n * high_n + mid_i * high_n + high_i) * per_chunk + row_ids % per_chunk
    weights_all = tile_weights[0, 0]
    live = tile_count[0, 0].reshape(1)
    source = doubling_gather(features, "row", row_n)
    source_tiles = source.reshape(col_tiles, tile_len, width)
    summed = slot_pass(live, placed, col_ids, weights_all, source_tiles, row_tiles, scale, False)
    partial_value = summed.reshape(row_len, width)
    partial_value = pair_scatter(partial_value, "core")
    partial_value = lax.psum_scatter(partial_value, "mid", scatter_dimension=0, tiled=True)
    partial_value = pair_scatter(partial_value, "high")
    aggregate = partial_value.astype(jnp.bfloat16)
    hidden, grad_own = dense_layer(aggregate, weight, cotangent)
    weight_part = lax.dot_general(
        aggregate, grad_own, (((0,), (0,)), ((), ())), preferred_element_type=jnp.float32
    )
    grad_agg = jnp.dot(grad_own, weight.T, preferred_element_type=jnp.float32).astype(jnp.bfloat16)
    grad_source, weight_sum = carried_gather(grad_agg, weight_part, "high", high_n)
    grad_source, weight_sum = carried_gather(grad_source, weight_sum, "mid", mid_n)
    grad_source, weight_sum = carried_gather(grad_source, weight_sum, "core", core_n)
    grad_tiles = grad_source.reshape(row_tiles, tile_len, width)
    back_summed = slot_pass(live, placed, col_ids, weights_all, grad_tiles, col_tiles, scale, True)
    back_partial = back_summed.reshape(col_len, width)
    back_value, weight_sum = carried_scatter(back_partial, weight_sum, "row", row_n)
    feature_grad = back_value.astype(jnp.bfloat16)
    weight_grad = weight_sum / math.sqrt(nodes_all)
    return (hidden, weight_grad, feature_grad)


def solution(mesh):
    row_n, col_n = mesh.shape["row"], mesh.shape["col"]
    core_n = 2
    high_n = 2
    mid_n = col_n // (high_n * core_n)
    sizes = (row_n, high_n, mid_n, core_n)
    fine = Mesh(mesh.devices.reshape(sizes), ("row", "high", "mid", "core"))
    col = ("high", "mid", "core")
    in_specs = (
        P(col + ("row",), None),
        P(),
        P(("row",) + col, None),
        P("row", col, None),
        P("row", col, None),
        P("row", col, None, None, None),
        P("row", col),
    )
    out_specs = (P(("row",) + col, None), P(), P(col + ("row",), None))
    return jax.shard_map(
        functools.partial(on_device, sizes=sizes),
        mesh=fine,
        in_specs=in_specs,
        out_specs=out_specs,
        check_vma=False,
    )
```

```python
import functools
import math

import jax
import jax.numpy as jnp
from jax import lax
from jax.experimental import pallas as pl
from jax.experimental.pallas import tpu as pltpu
from jax.sharding import Mesh
from jax.sharding import PartitionSpec as P

SPARSITY = 128


def slot_kernel(live_ref, rows_ref, cols_ref, tiles_ref, src_ref, out_ref, *, per_block, scale, transpose):
    block_id = pl.program_id(0)

    @pl.when(block_id == 0)
    def _():
        out_ref[...] = jnp.zeros_like(out_ref)

    live = live_ref[0]
    for k in range(per_block):
        slot = block_id * per_block + k

        @pl.when(slot < live)
        def _():
            tile_vals = tiles_ref[k].astype(jnp.bfloat16)
            if transpose:
                piece = src_ref[rows_ref[slot]]
                product = lax.dot_general(
                    tile_vals, piece, (((0,), (0,)), ((), ())), preferred_element_type=jnp.float32
                )
                target = cols_ref[slot]
            else:
                piece = src_ref[cols_ref[slot]]
                product = jnp.dot(tile_vals, piece, preferred_element_type=jnp.float32)
                target = rows_ref[slot]
            out_ref[target] += product

    @pl.when(block_id == pl.num_programs(0) - 1)
    def _():
        out_ref[...] = out_ref[...] * scale


def slot_pass(live, row_ids, col_ids, tiles, source_tiles, out_tiles, scale, transpose):
    slot_total, tile_len, _ = tiles.shape
    width = source_tiles.shape[-1]
    per_block = math.gcd(slot_total, 16)

    def tile_block(block_id, live_ref, rows_ref, cols_ref):
        last = jnp.maximum(live_ref[0] - 1, 0) // per_block
        return (jnp.minimum(block_id, last), 0, 0)

    def whole(block_id, live_ref, rows_ref, cols_ref):
        return (0, 0, 0)

    grid_spec = pltpu.PrefetchScalarGridSpec(
        num_scalar_prefetch=3,
        grid=(slot_total // per_block,),
        in_specs=[
            pl.BlockSpec((per_block, tile_len, tile_len), tile_block),
            pl.BlockSpec(source_tiles.shape, whole),
        ],
        out_specs=pl.BlockSpec((out_tiles, tile_len, width), whole),
    )
    return pl.pallas_call(
        functools.partial(slot_kernel, per_block=per_block, scale=scale, transpose=transpose),
        grid_spec=grid_spec,
        out_shape=jax.ShapeDtypeStruct((out_tiles, tile_len, width), jnp.float32),
        compiler_params=pltpu.CompilerParams(
            dimension_semantics=("arbitrary",), vmem_limit_bytes=48 * 1024 * 1024
        ),
    )(live, row_ids, col_ids, tiles, source_tiles)


def dense_layer(aggregate, weight, cotangent):
    preact = jnp.dot(aggregate, weight, preferred_element_type=jnp.float32)
    hidden = jax.nn.silu(preact).astype(jnp.bfloat16)
    sigma = jax.nn.sigmoid(preact)
    grad_pre = (cotangent.astype(jnp.float32) * sigma * (1.0 + preact * (1.0 - sigma))).astype(
        jnp.bfloat16
    )
    return (hidden, grad_pre)


def butterfly_sum(value, axes, count, levels):
    for level in levels:
        pairs = [(i, i ^ (1 << level)) for i in range(count)]
        value = value + lax.ppermute(value, axes, pairs)
    return value


def doubling_gather(value, axis, count):
    own = lax.axis_index(axis)
    for level in range(count.bit_length() - 1):
        pairs = [(i, i ^ (1 << level)) for i in range(count)]
        other = lax.ppermute(value, axis, pairs)
        low = ((own >> level) & 1) == 0
        value = jnp.concatenate(
            [jnp.where(low, value, other), jnp.where(low, other, value)], axis=0
        )
    return value


def pair_scatter(value, axis):
    half = value.shape[0] // 2
    own = lax.axis_index(axis)
    keep = lax.dynamic_slice_in_dim(value, own * half, half, 0)
    send = lax.dynamic_slice_in_dim(value, (1 - own) * half, half, 0)
    return keep + lax.ppermute(send, axis, [(0, 1), (1, 0)])


def pair_gather(value, axis):
    own = lax.axis_index(axis)
    other = lax.ppermute(value, axis, [(0, 1), (1, 0)])
    first = jnp.where(own == 0, value, other)
    second = jnp.where(own == 0, other, value)
    return jnp.concatenate([first, second], axis=0)


def on_device(
    features, weight, cotangent, tile_rows, tile_cols, tile_weights, tile_count, *, sizes
):
    row_n, high_n, mid_n, core_n = sizes
    col_axes = ("high", "mid", "core")
    col_n = high_n * mid_n * core_n
    node_dev = cotangent.shape[0]
    width = features.shape[1]
    slot_total = tile_weights.shape[2]
    tile_len = tile_weights.shape[-1]
    sparsity_value = SPARSITY
    fan_value = slot_total * tile_len * tile_len // (node_dev * sparsity_value)
    scale = 1.0 / math.sqrt(2.0 * fan_value)
    row_len = node_dev * col_n
    col_len = node_dev * row_n
    row_tiles = row_len // tile_len
    col_tiles = col_len // tile_len
    nodes_all = row_len * row_n
    per_chunk = node_dev // tile_len
    row_ids = tile_rows[0, 0]
    col_ids = tile_cols[0, 0]
    chunk = row_ids // per_chunk
    high_i = chunk // (mid_n * core_n)
    mid_i = (chunk // core_n) % mid_n
    core_i = chunk % core_n
    placed = (core_i * mid_n * high_n + mid_i * high_n + high_i) * per_chunk + row_ids % per_chunk
    weights_all = tile_weights[0, 0]
    live = tile_count[0, 0].reshape(1)
    source = doubling_gather(features, "row", row_n)
    source_tiles = source.reshape(col_tiles, tile_len, width)
    summed = slot_pass(live, placed, col_ids, weights_all, source_tiles, row_tiles, scale, False)
    partial_value = summed.reshape(row_len, width)
    partial_value = pair_scatter(partial_value, "core")
    partial_value = lax.psum_scatter(partial_value, "mid", scatter_dimension=0, tiled=True)
    partial_value = pair_scatter(partial_value, "high")
    aggregate = partial_value.astype(jnp.bfloat16)
    hidden, grad_own = dense_layer(aggregate, weight, cotangent)
    weight_part = lax.dot_general(
        aggregate, grad_own, (((0,), (0,)), ((), ())), preferred_element_type=jnp.float32
    )
    grad_agg = jnp.dot(grad_own, weight.T, preferred_element_type=jnp.float32).astype(jnp.bfloat16)
    every = ("row",) + col_axes
    levels = list(range((row_n * col_n).bit_length() - 1))
    weight_sum = butterfly_sum(weight_part, every, row_n * col_n, levels)
    grad_source = pair_gather(grad_agg, "high")
    grad_source = lax.all_gather(grad_source, "mid", axis=0, tiled=True)
    grad_source = pair_gather(grad_source, "core")
    grad_tiles = grad_source.reshape(row_tiles, tile_len, width)
    back_summed = slot_pass(live, placed, col_ids, weights_all, grad_tiles, col_tiles, scale, True)
    back_partial = back_summed.reshape(col_len, width)
    feature_grad = lax.psum_scatter(back_partial, "row", scatter_dimension=0, tiled=True).astype(
        jnp.bfloat16
    )
    weight_grad = weight_sum / math.sqrt(nodes_all)
    return (hidden, weight_grad, feature_grad)


def solution(mesh):
    row_n, col_n = mesh.shape["row"], mesh.shape["col"]
    core_n = 2
    high_n = 2
    mid_n = col_n // (high_n * core_n)
    sizes = (row_n, high_n, mid_n, core_n)
    fine = Mesh(mesh.devices.reshape(sizes), ("row", "high", "mid", "core"))
    col = ("high", "mid", "core")
    in_specs = (
        P(col + ("row",), None),
        P(),
        P(("row",) + col, None),
        P("row", col, None),
        P("row", col, None),
        P("row", col, None, None, None),
        P("row", col),
    )
    out_specs = (P(("row",) + col, None), P(), P(col + ("row",), None))
    return jax.shard_map(
        functools.partial(on_device, sizes=sizes),
        mesh=fine,
        in_specs=in_specs,
        out_specs=out_specs,
        check_vma=False,
    )
```

```python
import functools
import math

import jax
import jax.numpy as jnp
from jax import lax
from jax.experimental import pallas as pl
from jax.experimental.pallas import tpu as pltpu
from jax.sharding import Mesh
from jax.sharding import PartitionSpec as P

SPARSITY = 128


def slot_kernel(live_ref, rows_ref, cols_ref, tiles_ref, src_ref, out_ref, *, per_block, scale, transpose):
    block_id = pl.program_id(0)

    @pl.when(block_id == 0)
    def _():
        out_ref[...] = jnp.zeros_like(out_ref)

    live = live_ref[0]
    for k in range(per_block):
        slot = block_id * per_block + k

        @pl.when(slot < live)
        def _():
            tile_vals = tiles_ref[k].astype(jnp.bfloat16)
            if transpose:
                piece = src_ref[rows_ref[slot]]
                product = lax.dot_general(
                    tile_vals, piece, (((0,), (0,)), ((), ())), preferred_element_type=jnp.float32
                )
                target = cols_ref[slot]
            else:
                piece = src_ref[cols_ref[slot]]
                product = jnp.dot(tile_vals, piece, preferred_element_type=jnp.float32)
                target = rows_ref[slot]
            out_ref[target] += product

    @pl.when(block_id == pl.num_programs(0) - 1)
    def _():
        out_ref[...] = out_ref[...] * scale


def slot_pass(live, row_ids, col_ids, tiles, source_tiles, out_tiles, scale, transpose):
    slot_total, tile_len, _ = tiles.shape
    width = source_tiles.shape[-1]
    per_block = math.gcd(slot_total, 16)

    def tile_block(block_id, live_ref, rows_ref, cols_ref):
        last = jnp.maximum(live_ref[0] - 1, 0) // per_block
        return (jnp.minimum(block_id, last), 0, 0)

    def whole(block_id, live_ref, rows_ref, cols_ref):
        return (0, 0, 0)

    grid_spec = pltpu.PrefetchScalarGridSpec(
        num_scalar_prefetch=3,
        grid=(slot_total // per_block,),
        in_specs=[
            pl.BlockSpec((per_block, tile_len, tile_len), tile_block),
            pl.BlockSpec(source_tiles.shape, whole),
        ],
        out_specs=pl.BlockSpec((out_tiles, tile_len, width), whole),
    )
    return pl.pallas_call(
        functools.partial(slot_kernel, per_block=per_block, scale=scale, transpose=transpose),
        grid_spec=grid_spec,
        out_shape=jax.ShapeDtypeStruct((out_tiles, tile_len, width), jnp.float32),
        compiler_params=pltpu.CompilerParams(
            dimension_semantics=("arbitrary",), vmem_limit_bytes=48 * 1024 * 1024
        ),
    )(live, row_ids, col_ids, tiles, source_tiles)


def dense_layer(aggregate, weight, cotangent):
    preact = jnp.dot(aggregate, weight, preferred_element_type=jnp.float32)
    hidden = jax.nn.silu(preact).astype(jnp.bfloat16)
    sigma = jax.nn.sigmoid(preact)
    grad_pre = (cotangent.astype(jnp.float32) * sigma * (1.0 + preact * (1.0 - sigma))).astype(
        jnp.bfloat16
    )
    return (hidden, grad_pre)


def butterfly_sum(value, axes, count, levels):
    for level in levels:
        pairs = [(i, i ^ (1 << level)) for i in range(count)]
        value = value + lax.ppermute(value, axes, pairs)
    return value


def doubling_gather(value, axis, count):
    own = lax.axis_index(axis)
    for level in range(count.bit_length() - 1):
        pairs = [(i, i ^ (1 << level)) for i in range(count)]
        other = lax.ppermute(value, axis, pairs)
        low = ((own >> level) & 1) == 0
        value = jnp.concatenate(
            [jnp.where(low, value, other), jnp.where(low, other, value)], axis=0
        )
    return value


def pair_scatter(value, axis):
    half = value.shape[0] // 2
    own = lax.axis_index(axis)
    keep = lax.dynamic_slice_in_dim(value, own * half, half, 0)
    send = lax.dynamic_slice_in_dim(value, (1 - own) * half, half, 0)
    return keep + lax.ppermute(send, axis, [(0, 1), (1, 0)])


def pair_gather(value, axis):
    own = lax.axis_index(axis)
    other = lax.ppermute(value, axis, [(0, 1), (1, 0)])
    first = jnp.where(own == 0, value, other)
    second = jnp.where(own == 0, other, value)
    return jnp.concatenate([first, second], axis=0)


def split_scatter(value, axis, count):
    chunk = value.shape[0] // count
    blocks = value.reshape(count, chunk, value.shape[1])
    first = blocks[:, : chunk // 2].reshape(count * (chunk // 2), value.shape[1])
    second = blocks[:, chunk // 2 :]
    first = lax.psum_scatter(first, axis, scatter_dimension=0, tiled=True)
    second = lax.all_to_all(second, axis, 0, 0, tiled=False).sum(0)
    return jnp.concatenate([first, second], axis=0)


def on_device(
    features, weight, cotangent, tile_rows, tile_cols, tile_weights, tile_count, *, sizes
):
    row_n, high_n, mid_n, core_n = sizes
    col_axes = ("high", "mid", "core")
    col_n = high_n * mid_n * core_n
    node_dev = cotangent.shape[0]
    width = features.shape[1]
    slot_total = tile_weights.shape[2]
    tile_len = tile_weights.shape[-1]
    sparsity_value = SPARSITY
    fan_value = slot_total * tile_len * tile_len // (node_dev * sparsity_value)
    scale = 1.0 / math.sqrt(2.0 * fan_value)
    row_len = node_dev * col_n
    col_len = node_dev * row_n
    row_tiles = row_len // tile_len
    col_tiles = col_len // tile_len
    nodes_all = row_len * row_n
    per_chunk = node_dev // tile_len
    row_ids = tile_rows[0, 0]
    col_ids = tile_cols[0, 0]
    chunk = row_ids // per_chunk
    high_i = chunk // (mid_n * core_n)
    mid_i = (chunk // core_n) % mid_n
    core_i = chunk % core_n
    placed = (core_i * mid_n * high_n + mid_i * high_n + high_i) * per_chunk + row_ids % per_chunk
    weights_all = tile_weights[0, 0]
    live = tile_count[0, 0].reshape(1)
    source = doubling_gather(features, "row", row_n)
    source_tiles = source.reshape(col_tiles, tile_len, width)
    summed = slot_pass(live, placed, col_ids, weights_all, source_tiles, row_tiles, scale, False)
    partial_value = summed.reshape(row_len, width)
    partial_value = pair_scatter(partial_value, "core")
    partial_value = split_scatter(partial_value, "mid", mid_n)
    partial_value = pair_scatter(partial_value, "high")
    aggregate = partial_value.astype(jnp.bfloat16)
    hidden, grad_own = dense_layer(aggregate, weight, cotangent)
    weight_part = lax.dot_general(
        aggregate, grad_own, (((0,), (0,)), ((), ())), preferred_element_type=jnp.float32
    )
    grad_agg = jnp.dot(grad_own, weight.T, preferred_element_type=jnp.float32).astype(jnp.bfloat16)
    every = ("row",) + col_axes
    levels = list(range((row_n * col_n).bit_length() - 1))
    weight_sum = butterfly_sum(weight_part, every, row_n * col_n, levels)
    grad_source = pair_gather(grad_agg, "high")
    grad_source = lax.all_gather(grad_source, "mid", axis=0, tiled=True)
    grad_source = pair_gather(grad_source, "core")
    grad_tiles = grad_source.reshape(row_tiles, tile_len, width)
    back_summed = slot_pass(live, placed, col_ids, weights_all, grad_tiles, col_tiles, scale, True)
    back_partial = back_summed.reshape(col_len, width)
    feature_grad = lax.psum_scatter(back_partial, "row", scatter_dimension=0, tiled=True).astype(
        jnp.bfloat16
    )
    weight_grad = weight_sum / math.sqrt(nodes_all)
    return (hidden, weight_grad, feature_grad)


def solution(mesh):
    row_n, col_n = mesh.shape["row"], mesh.shape["col"]
    core_n = 2
    high_n = 2
    mid_n = col_n // (high_n * core_n)
    sizes = (row_n, high_n, mid_n, core_n)
    fine = Mesh(mesh.devices.reshape(sizes), ("row", "high", "mid", "core"))
    col = ("high", "mid", "core")
    in_specs = (
        P(col + ("row",), None),
        P(),
        P(("row",) + col, None),
        P("row", col, None),
        P("row", col, None),
        P("row", col, None, None, None),
        P("row", col),
    )
    out_specs = (P(("row",) + col, None), P(), P(col + ("row",), None))
    return jax.shard_map(
        functools.partial(on_device, sizes=sizes),
        mesh=fine,
        in_specs=in_specs,
        out_specs=out_specs,
        check_vma=False,
    )
```

```python
import functools
import math

import jax
import jax.numpy as jnp
from jax import lax
from jax.experimental import pallas as pl
from jax.experimental.pallas import tpu as pltpu
from jax.sharding import Mesh
from jax.sharding import PartitionSpec as P

SPARSITY = 128


def slot_kernel(live_ref, rows_ref, cols_ref, tiles_ref, src_ref, out_ref, *, per_block, scale, transpose):
    block_id = pl.program_id(0)

    @pl.when(block_id == 0)
    def _():
        out_ref[...] = jnp.zeros_like(out_ref)

    live = live_ref[0]
    for k in range(per_block):
        slot = block_id * per_block + k

        @pl.when(slot < live)
        def _():
            tile_vals = tiles_ref[k].astype(jnp.bfloat16)
            if transpose:
                piece = src_ref[rows_ref[slot]]
                product = lax.dot_general(
                    tile_vals, piece, (((0,), (0,)), ((), ())), preferred_element_type=jnp.float32
                )
                target = cols_ref[slot]
            else:
                piece = src_ref[cols_ref[slot]]
                product = jnp.dot(tile_vals, piece, preferred_element_type=jnp.float32)
                target = rows_ref[slot]
            out_ref[target] += product

    @pl.when(block_id == pl.num_programs(0) - 1)
    def _():
        out_ref[...] = out_ref[...] * scale


def slot_pass(live, row_ids, col_ids, tiles, source_tiles, out_tiles, scale, transpose):
    slot_total, tile_len, _ = tiles.shape
    width = source_tiles.shape[-1]
    per_block = math.gcd(slot_total, 16)

    def tile_block(block_id, live_ref, rows_ref, cols_ref):
        last = jnp.maximum(live_ref[0] - 1, 0) // per_block
        return (jnp.minimum(block_id, last), 0, 0)

    def whole(block_id, live_ref, rows_ref, cols_ref):
        return (0, 0, 0)

    grid_spec = pltpu.PrefetchScalarGridSpec(
        num_scalar_prefetch=3,
        grid=(slot_total // per_block,),
        in_specs=[
            pl.BlockSpec((per_block, tile_len, tile_len), tile_block),
            pl.BlockSpec(source_tiles.shape, whole),
        ],
        out_specs=pl.BlockSpec((out_tiles, tile_len, width), whole),
    )
    return pl.pallas_call(
        functools.partial(slot_kernel, per_block=per_block, scale=scale, transpose=transpose),
        grid_spec=grid_spec,
        out_shape=jax.ShapeDtypeStruct((out_tiles, tile_len, width), jnp.float32),
        compiler_params=pltpu.CompilerParams(
            dimension_semantics=("arbitrary",), vmem_limit_bytes=48 * 1024 * 1024
        ),
    )(live, row_ids, col_ids, tiles, source_tiles)


def dense_layer(aggregate, weight, cotangent):
    preact = jnp.dot(aggregate, weight, preferred_element_type=jnp.float32)
    hidden = jax.nn.silu(preact).astype(jnp.bfloat16)
    sigma = jax.nn.sigmoid(preact)
    grad_pre = (cotangent.astype(jnp.float32) * sigma * (1.0 + preact * (1.0 - sigma))).astype(
        jnp.bfloat16
    )
    return (hidden, grad_pre)


def butterfly_sum(value, axes, count, levels):
    for level in levels:
        pairs = [(i, i ^ (1 << level)) for i in range(count)]
        value = value + lax.ppermute(value, axes, pairs)
    return value


def doubling_gather(value, axis, count):
    own = lax.axis_index(axis)
    for level in range(count.bit_length() - 1):
        pairs = [(i, i ^ (1 << level)) for i in range(count)]
        other = lax.ppermute(value, axis, pairs)
        low = ((own >> level) & 1) == 0
        value = jnp.concatenate(
            [jnp.where(low, value, other), jnp.where(low, other, value)], axis=0
        )
    return value


def pair_scatter(value, axis):
    half = value.shape[0] // 2
    own = lax.axis_index(axis)
    keep = lax.dynamic_slice_in_dim(value, own * half, half, 0)
    send = lax.dynamic_slice_in_dim(value, (1 - own) * half, half, 0)
    return keep + lax.ppermute(send, axis, [(0, 1), (1, 0)])


def pair_gather(value, axis):
    own = lax.axis_index(axis)
    other = lax.ppermute(value, axis, [(0, 1), (1, 0)])
    first = jnp.where(own == 0, value, other)
    second = jnp.where(own == 0, other, value)
    return jnp.concatenate([first, second], axis=0)


def on_device(
    features, weight, cotangent, tile_rows, tile_cols, tile_weights, tile_count, *, sizes
):
    row_n, high_n, mid_n, core_n = sizes
    col_axes = ("high", "mid", "core")
    col_n = high_n * mid_n * core_n
    node_dev = cotangent.shape[0]
    width = features.shape[1]
    slot_total = tile_weights.shape[2]
    tile_len = tile_weights.shape[-1]
    sparsity_value = SPARSITY
    fan_value = slot_total * tile_len * tile_len // (node_dev * sparsity_value)
    scale = 1.0 / math.sqrt(2.0 * fan_value)
    row_len = node_dev * col_n
    col_len = node_dev * row_n
    row_tiles = row_len // tile_len
    col_tiles = col_len // tile_len
    nodes_all = row_len * row_n
    per_chunk = node_dev // tile_len
    row_ids = tile_rows[0, 0]
    col_ids = tile_cols[0, 0]
    chunk = row_ids // per_chunk
    high_i = chunk // (mid_n * core_n)
    mid_i = (chunk // core_n) % mid_n
    core_i = chunk % core_n
    placed = (core_i * mid_n * high_n + mid_i * high_n + high_i) * per_chunk + row_ids % per_chunk
    kept = (core_i == lax.axis_index("core")).astype(jnp.int32)
    fwd_placed = (kept * mid_n * high_n + mid_i * high_n + high_i) * per_chunk + row_ids % per_chunk
    weights_all = tile_weights[0, 0]
    live = tile_count[0, 0].reshape(1)
    source = doubling_gather(features, "row", row_n)
    source_tiles = source.reshape(col_tiles, tile_len, width)
    summed = slot_pass(live, fwd_placed, col_ids, weights_all, source_tiles, row_tiles, scale, False)
    partial_value = summed.reshape(row_len, width)
    half = row_len // 2
    partial_value = partial_value[half:] + lax.ppermute(
        partial_value[:half], "core", [(0, 1), (1, 0)]
    )
    partial_value = lax.psum_scatter(partial_value, "mid", scatter_dimension=0, tiled=True)
    partial_value = pair_scatter(partial_value, "high")
    aggregate = partial_value.astype(jnp.bfloat16)
    hidden, grad_own = dense_layer(aggregate, weight, cotangent)
    weight_part = lax.dot_general(
        aggregate, grad_own, (((0,), (0,)), ((), ())), preferred_element_type=jnp.float32
    )
    grad_agg = jnp.dot(grad_own, weight.T, preferred_element_type=jnp.float32).astype(jnp.bfloat16)
    every = ("row",) + col_axes
    levels = list(range((row_n * col_n).bit_length() - 1))
    weight_sum = butterfly_sum(weight_part, every, row_n * col_n, levels)
    grad_source = pair_gather(grad_agg, "high")
    grad_source = lax.all_gather(grad_source, "mid", axis=0, tiled=True)
    grad_source = pair_gather(grad_source, "core")
    grad_tiles = grad_source.reshape(row_tiles, tile_len, width)
    back_summed = slot_pass(live, placed, col_ids, weights_all, grad_tiles, col_tiles, scale, True)
    back_partial = back_summed.reshape(col_len, width)
    feature_grad = lax.psum_scatter(back_partial, "row", scatter_dimension=0, tiled=True).astype(
        jnp.bfloat16
    )
    weight_grad = weight_sum / math.sqrt(nodes_all)
    return (hidden, weight_grad, feature_grad)


def solution(mesh):
    row_n, col_n = mesh.shape["row"], mesh.shape["col"]
    core_n = 2
    high_n = 2
    mid_n = col_n // (high_n * core_n)
    sizes = (row_n, high_n, mid_n, core_n)
    fine = Mesh(mesh.devices.reshape(sizes), ("row", "high", "mid", "core"))
    col = ("high", "mid", "core")
    in_specs = (
        P(col + ("row",), None),
        P(),
        P(("row",) + col, None),
        P("row", col, None),
        P("row", col, None),
        P("row", col, None, None, None),
        P("row", col),
    )
    out_specs = (P(("row",) + col, None), P(), P(col + ("row",), None))
    return jax.shard_map(
        functools.partial(on_device, sizes=sizes),
        mesh=fine,
        in_specs=in_specs,
        out_specs=out_specs,
        check_vma=False,
    )
```

```python
import functools
import math

import jax
import jax.numpy as jnp
from jax import lax
from jax.experimental import pallas as pl
from jax.experimental.pallas import tpu as pltpu
from jax.sharding import Mesh
from jax.sharding import PartitionSpec as P

SPARSITY = 128


def slot_kernel(live_ref, rows_ref, cols_ref, tiles_ref, src_ref, out_ref, *, per_block, scale, transpose):
    block_id = pl.program_id(0)

    @pl.when(block_id == 0)
    def _():
        out_ref[...] = jnp.zeros_like(out_ref)

    live = live_ref[0]
    for k in range(per_block):
        slot = block_id * per_block + k

        @pl.when(slot < live)
        def _():
            tile_vals = tiles_ref[k].astype(jnp.bfloat16)
            if transpose:
                piece = src_ref[rows_ref[slot]]
                product = lax.dot_general(
                    tile_vals, piece, (((0,), (0,)), ((), ())), preferred_element_type=jnp.float32
                )
                target = cols_ref[slot]
            else:
                piece = src_ref[cols_ref[slot]]
                product = jnp.dot(tile_vals, piece, preferred_element_type=jnp.float32)
                target = rows_ref[slot]
            out_ref[target] += product

    @pl.when(block_id == pl.num_programs(0) - 1)
    def _():
        out_ref[...] = out_ref[...] * scale


def back_kernel(
    live_ref, rows_ref, cols_ref, halves_ref, tiles_ref, own_ref, other_ref, out_ref, *,
    per_block, scale
):
    block_id = pl.program_id(0)

    @pl.when(block_id == 0)
    def _():
        out_ref[...] = jnp.zeros_like(out_ref)

    live = live_ref[0]
    for k in range(per_block):
        slot = block_id * per_block + k
        for half, half_ref in ((0, own_ref), (1, other_ref)):

            @pl.when((slot < live) & (halves_ref[slot] == half))
            def _(half_ref=half_ref):
                tile_vals = tiles_ref[k].astype(jnp.bfloat16)
                piece = half_ref[rows_ref[slot]]
                product = lax.dot_general(
                    tile_vals, piece, (((0,), (0,)), ((), ())), preferred_element_type=jnp.float32
                )
                out_ref[cols_ref[slot]] += product

    @pl.when(block_id == pl.num_programs(0) - 1)
    def _():
        out_ref[...] = out_ref[...] * scale


def slot_pass(live, row_ids, col_ids, tiles, source_tiles, out_tiles, scale, transpose):
    slot_total, tile_len, _ = tiles.shape
    width = source_tiles.shape[-1]
    per_block = math.gcd(slot_total, 16)

    def tile_block(block_id, live_ref, rows_ref, cols_ref):
        last = jnp.maximum(live_ref[0] - 1, 0) // per_block
        return (jnp.minimum(block_id, last), 0, 0)

    def whole(block_id, live_ref, rows_ref, cols_ref):
        return (0, 0, 0)

    grid_spec = pltpu.PrefetchScalarGridSpec(
        num_scalar_prefetch=3,
        grid=(slot_total // per_block,),
        in_specs=[
            pl.BlockSpec((per_block, tile_len, tile_len), tile_block),
            pl.BlockSpec(source_tiles.shape, whole),
        ],
        out_specs=pl.BlockSpec((out_tiles, tile_len, width), whole),
    )
    return pl.pallas_call(
        functools.partial(slot_kernel, per_block=per_block, scale=scale, transpose=transpose),
        grid_spec=grid_spec,
        out_shape=jax.ShapeDtypeStruct((out_tiles, tile_len, width), jnp.float32),
        compiler_params=pltpu.CompilerParams(
            dimension_semantics=("arbitrary",), vmem_limit_bytes=48 * 1024 * 1024
        ),
    )(live, row_ids, col_ids, tiles, source_tiles)


def back_pass(live, row_ids, col_ids, halves, tiles, own_tiles, other_tiles, out_tiles, scale):
    slot_total, tile_len, _ = tiles.shape
    width = own_tiles.shape[-1]
    per_block = math.gcd(slot_total, 16)

    def tile_block(block_id, live_ref, rows_ref, cols_ref, halves_ref):
        last = jnp.maximum(live_ref[0] - 1, 0) // per_block
        return (jnp.minimum(block_id, last), 0, 0)

    def whole(block_id, live_ref, rows_ref, cols_ref, halves_ref):
        return (0, 0, 0)

    grid_spec = pltpu.PrefetchScalarGridSpec(
        num_scalar_prefetch=4,
        grid=(slot_total // per_block,),
        in_specs=[
            pl.BlockSpec((per_block, tile_len, tile_len), tile_block),
            pl.BlockSpec(own_tiles.shape, whole),
            pl.BlockSpec(other_tiles.shape, whole),
        ],
        out_specs=pl.BlockSpec((out_tiles, tile_len, width), whole),
    )
    return pl.pallas_call(
        functools.partial(back_kernel, per_block=per_block, scale=scale),
        grid_spec=grid_spec,
        out_shape=jax.ShapeDtypeStruct((out_tiles, tile_len, width), jnp.float32),
        compiler_params=pltpu.CompilerParams(
            dimension_semantics=("arbitrary",), vmem_limit_bytes=48 * 1024 * 1024
        ),
    )(live, row_ids, col_ids, halves, tiles, own_tiles, other_tiles)


def dense_layer(aggregate, weight, cotangent):
    preact = jnp.dot(aggregate, weight, preferred_element_type=jnp.float32)
    hidden = jax.nn.silu(preact).astype(jnp.bfloat16)
    sigma = jax.nn.sigmoid(preact)
    grad_pre = (cotangent.astype(jnp.float32) * sigma * (1.0 + preact * (1.0 - sigma))).astype(
        jnp.bfloat16
    )
    return (hidden, grad_pre)


def butterfly_sum(value, axes, count, levels):
    for level in levels:
        pairs = [(i, i ^ (1 << level)) for i in range(count)]
        value = value + lax.ppermute(value, axes, pairs)
    return value


def doubling_gather(value, axis, count):
    own = lax.axis_index(axis)
    for level in range(count.bit_length() - 1):
        pairs = [(i, i ^ (1 << level)) for i in range(count)]
        other = lax.ppermute(value, axis, pairs)
        low = ((own >> level) & 1) == 0
        value = jnp.concatenate(
            [jnp.where(low, value, other), jnp.where(low, other, value)], axis=0
        )
    return value


def pair_scatter(value, axis):
    half = value.shape[0] // 2
    own = lax.axis_index(axis)
    keep = lax.dynamic_slice_in_dim(value, own * half, half, 0)
    send = lax.dynamic_slice_in_dim(value, (1 - own) * half, half, 0)
    return keep + lax.ppermute(send, axis, [(0, 1), (1, 0)])


def pair_gather(value, axis):
    own = lax.axis_index(axis)
    other = lax.ppermute(value, axis, [(0, 1), (1, 0)])
    first = jnp.where(own == 0, value, other)
    second = jnp.where(own == 0, other, value)
    return jnp.concatenate([first, second], axis=0)


def on_device(
    features, weight, cotangent, tile_rows, tile_cols, tile_weights, tile_count, *, sizes
):
    row_n, high_n, mid_n, core_n = sizes
    col_axes = ("high", "mid", "core")
    col_n = high_n * mid_n * core_n
    node_dev = cotangent.shape[0]
    width = features.shape[1]
    slot_total = tile_weights.shape[2]
    tile_len = tile_weights.shape[-1]
    sparsity_value = SPARSITY
    fan_value = slot_total * tile_len * tile_len // (node_dev * sparsity_value)
    scale = 1.0 / math.sqrt(2.0 * fan_value)
    row_len = node_dev * col_n
    col_len = node_dev * row_n
    row_tiles = row_len // tile_len
    col_tiles = col_len // tile_len
    nodes_all = row_len * row_n
    per_chunk = node_dev // tile_len
    row_ids = tile_rows[0, 0]
    col_ids = tile_cols[0, 0]
    chunk = row_ids // per_chunk
    high_i = chunk // (mid_n * core_n)
    mid_i = (chunk // core_n) % mid_n
    core_i = chunk % core_n
    placed = (core_i * mid_n * high_n + mid_i * high_n + high_i) * per_chunk + row_ids % per_chunk
    kept = (core_i == lax.axis_index("core")).astype(jnp.int32)
    fwd_placed = (kept * mid_n * high_n + mid_i * high_n + high_i) * per_chunk + row_ids % per_chunk
    weights_all = tile_weights[0, 0]
    live = tile_count[0, 0].reshape(1)
    source = doubling_gather(features, "row", row_n)
    source_tiles = source.reshape(col_tiles, tile_len, width)
    summed = slot_pass(live, fwd_placed, col_ids, weights_all, source_tiles, row_tiles, scale, False)
    partial_value = summed.reshape(row_len, width)
    half = row_len // 2
    partial_value = partial_value[half:] + lax.ppermute(
        partial_value[:half], "core", [(0, 1), (1, 0)]
    )
    partial_value = lax.psum_scatter(partial_value, "mid", scatter_dimension=0, tiled=True)
    partial_value = pair_scatter(partial_value, "high")
    aggregate = partial_value.astype(jnp.bfloat16)
    hidden, grad_own = dense_layer(aggregate, weight, cotangent)
    weight_part = lax.dot_general(
        aggregate, grad_own, (((0,), (0,)), ((), ())), preferred_element_type=jnp.float32
    )
    grad_agg = jnp.dot(grad_own, weight.T, preferred_element_type=jnp.float32).astype(jnp.bfloat16)
    every = ("row",) + col_axes
    levels = list(range((row_n * col_n).bit_length() - 1))
    weight_sum = butterfly_sum(weight_part, every, row_n * col_n, levels)
    grad_source = pair_gather(grad_agg, "high")
    grad_source = lax.all_gather(grad_source, "mid", axis=0, tiled=True)
    grad_other = lax.ppermute(grad_source, "core", [(0, 1), (1, 0)])
    half_tiles = row_tiles // core_n
    own_tiles = grad_source.reshape(half_tiles, tile_len, width)
    other_tiles = grad_other.reshape(half_tiles, tile_len, width)
    halves = (core_i != lax.axis_index("core")).astype(jnp.int32)
    back_summed = back_pass(
        live, placed % half_tiles, col_ids, halves, weights_all, own_tiles, other_tiles,
        col_tiles, scale,
    )
    back_partial = back_summed.reshape(col_len, width)
    feature_grad = lax.psum_scatter(back_partial, "row", scatter_dimension=0, tiled=True).astype(
        jnp.bfloat16
    )
    weight_grad = weight_sum / math.sqrt(nodes_all)
    return (hidden, weight_grad, feature_grad)


def solution(mesh):
    row_n, col_n = mesh.shape["row"], mesh.shape["col"]
    core_n = 2
    high_n = 2
    mid_n = col_n // (high_n * core_n)
    sizes = (row_n, high_n, mid_n, core_n)
    fine = Mesh(mesh.devices.reshape(sizes), ("row", "high", "mid", "core"))
    col = ("high", "mid", "core")
    in_specs = (
        P(col + ("row",), None),
        P(),
        P(("row",) + col, None),
        P("row", col, None),
        P("row", col, None),
        P("row", col, None, None, None),
        P("row", col),
    )
    out_specs = (P(("row",) + col, None), P(), P(col + ("row",), None))
    return jax.shard_map(
        functools.partial(on_device, sizes=sizes),
        mesh=fine,
        in_specs=in_specs,
        out_specs=out_specs,
        check_vma=False,
    )
```

```python
import functools
import math

import jax
import jax.numpy as jnp
from jax import lax
from jax.experimental import pallas as pl
from jax.experimental.pallas import tpu as pltpu
from jax.sharding import Mesh
from jax.sharding import PartitionSpec as P

SPARSITY = 128


def slot_kernel(live_ref, rows_ref, cols_ref, tiles_ref, src_ref, out_ref, *, per_block, scale, transpose):
    block_id = pl.program_id(0)

    @pl.when(block_id == 0)
    def _():
        out_ref[...] = jnp.zeros_like(out_ref)

    live = live_ref[0]
    for k in range(per_block):
        slot = block_id * per_block + k

        @pl.when(slot < live)
        def _():
            tile_vals = tiles_ref[k].astype(jnp.bfloat16)
            if transpose:
                piece = src_ref[rows_ref[slot]]
                product = lax.dot_general(
                    tile_vals, piece, (((0,), (0,)), ((), ())), preferred_element_type=jnp.float32
                )
                target = cols_ref[slot]
            else:
                piece = src_ref[cols_ref[slot]]
                product = jnp.dot(tile_vals, piece, preferred_element_type=jnp.float32)
                target = rows_ref[slot]
            out_ref[target] += product

    @pl.when(block_id == pl.num_programs(0) - 1)
    def _():
        out_ref[...] = out_ref[...] * scale


def back_kernel(
    live_ref, rows_ref, cols_ref, halves_ref, tiles_ref, own_ref, other_ref, out_ref, *,
    per_block, scale
):
    block_id = pl.program_id(0)

    @pl.when(block_id == 0)
    def _():
        out_ref[...] = jnp.zeros_like(out_ref)

    live = live_ref[0]
    for k in range(per_block):
        slot = block_id * per_block + k
        for half, half_ref in ((0, own_ref), (1, other_ref)):

            @pl.when((slot < live) & (halves_ref[slot] == half))
            def _(half_ref=half_ref):
                tile_vals = tiles_ref[k].astype(jnp.bfloat16)
                piece = half_ref[rows_ref[slot]]
                product = lax.dot_general(
                    tile_vals, piece, (((0,), (0,)), ((), ())), preferred_element_type=jnp.float32
                )
                out_ref[cols_ref[slot]] += product

    @pl.when(block_id == pl.num_programs(0) - 1)
    def _():
        out_ref[...] = out_ref[...] * scale


def slot_pass(live, row_ids, col_ids, tiles, source_tiles, out_tiles, scale, transpose):
    slot_total, tile_len, _ = tiles.shape
    width = source_tiles.shape[-1]
    per_block = math.gcd(slot_total, 16)

    def tile_block(block_id, live_ref, rows_ref, cols_ref):
        last = jnp.maximum(live_ref[0] - 1, 0) // per_block
        return (jnp.minimum(block_id, last), 0, 0)

    def whole(block_id, live_ref, rows_ref, cols_ref):
        return (0, 0, 0)

    grid_spec = pltpu.PrefetchScalarGridSpec(
        num_scalar_prefetch=3,
        grid=(slot_total // per_block,),
        in_specs=[
            pl.BlockSpec((per_block, tile_len, tile_len), tile_block),
            pl.BlockSpec(source_tiles.shape, whole),
        ],
        out_specs=pl.BlockSpec((out_tiles, tile_len, width), whole),
    )
    return pl.pallas_call(
        functools.partial(slot_kernel, per_block=per_block, scale=scale, transpose=transpose),
        grid_spec=grid_spec,
        out_shape=jax.ShapeDtypeStruct((out_tiles, tile_len, width), jnp.float32),
        compiler_params=pltpu.CompilerParams(
            dimension_semantics=("arbitrary",), vmem_limit_bytes=48 * 1024 * 1024
        ),
    )(live, row_ids, col_ids, tiles, source_tiles)


def back_pass(live, row_ids, col_ids, halves, tiles, own_tiles, other_tiles, out_tiles, scale):
    slot_total, tile_len, _ = tiles.shape
    width = own_tiles.shape[-1]
    per_block = math.gcd(slot_total, 16)

    def tile_block(block_id, live_ref, rows_ref, cols_ref, halves_ref):
        last = jnp.maximum(live_ref[0] - 1, 0) // per_block
        return (jnp.minimum(block_id, last), 0, 0)

    def whole(block_id, live_ref, rows_ref, cols_ref, halves_ref):
        return (0, 0, 0)

    grid_spec = pltpu.PrefetchScalarGridSpec(
        num_scalar_prefetch=4,
        grid=(slot_total // per_block,),
        in_specs=[
            pl.BlockSpec((per_block, tile_len, tile_len), tile_block),
            pl.BlockSpec(own_tiles.shape, whole),
            pl.BlockSpec(other_tiles.shape, whole),
        ],
        out_specs=pl.BlockSpec((out_tiles, tile_len, width), whole),
    )
    return pl.pallas_call(
        functools.partial(back_kernel, per_block=per_block, scale=scale),
        grid_spec=grid_spec,
        out_shape=jax.ShapeDtypeStruct((out_tiles, tile_len, width), jnp.float32),
        compiler_params=pltpu.CompilerParams(
            dimension_semantics=("arbitrary",), vmem_limit_bytes=48 * 1024 * 1024
        ),
    )(live, row_ids, col_ids, halves, tiles, own_tiles, other_tiles)


def dense_layer(aggregate, weight, cotangent):
    preact = jnp.dot(aggregate, weight, preferred_element_type=jnp.float32)
    hidden = jax.nn.silu(preact).astype(jnp.bfloat16)
    sigma = jax.nn.sigmoid(preact)
    grad_pre = (cotangent.astype(jnp.float32) * sigma * (1.0 + preact * (1.0 - sigma))).astype(
        jnp.bfloat16
    )
    return (hidden, grad_pre)


def butterfly_sum(value, axes, count, levels, ring_bits):
    low_bit, ring_n = ring_bits
    label = [p ^ (p >> 1) for p in range(ring_n)]
    position = {g: p for p, g in enumerate(label)}

    def partner(i, level):
        if low_bit <= level < low_bit + ring_n.bit_length() - 1:
            p = (i >> low_bit) % ring_n
            q = position[label[p] ^ (1 << (level - low_bit))]
            return i + ((q - p) << low_bit)
        return i ^ (1 << level)

    for level in levels:
        pairs = [(i, partner(i, level)) for i in range(count)]
        value = value + lax.ppermute(value, axes, pairs)
    return value


def doubling_gather(value, axis, count):
    own = lax.axis_index(axis)
    for level in range(count.bit_length() - 1):
        pairs = [(i, i ^ (1 << level)) for i in range(count)]
        other = lax.ppermute(value, axis, pairs)
        low = ((own >> level) & 1) == 0
        value = jnp.concatenate(
            [jnp.where(low, value, other), jnp.where(low, other, value)], axis=0
        )
    return value


def pair_scatter(value, axis):
    half = value.shape[0] // 2
    own = lax.axis_index(axis)
    keep = lax.dynamic_slice_in_dim(value, own * half, half, 0)
    send = lax.dynamic_slice_in_dim(value, (1 - own) * half, half, 0)
    return keep + lax.ppermute(send, axis, [(0, 1), (1, 0)])


def pair_gather(value, axis):
    own = lax.axis_index(axis)
    other = lax.ppermute(value, axis, [(0, 1), (1, 0)])
    first = jnp.where(own == 0, value, other)
    second = jnp.where(own == 0, other, value)
    return jnp.concatenate([first, second], axis=0)


def on_device(
    features, weight, cotangent, tile_rows, tile_cols, tile_weights, tile_count, *, sizes
):
    row_n, high_n, mid_n, core_n = sizes
    col_axes = ("high", "mid", "core")
    col_n = high_n * mid_n * core_n
    node_dev = cotangent.shape[0]
    width = features.shape[1]
    slot_total = tile_weights.shape[2]
    tile_len = tile_weights.shape[-1]
    sparsity_value = SPARSITY
    fan_value = slot_total * tile_len * tile_len // (node_dev * sparsity_value)
    scale = 1.0 / math.sqrt(2.0 * fan_value)
    row_len = node_dev * col_n
    col_len = node_dev * row_n
    row_tiles = row_len // tile_len
    col_tiles = col_len // tile_len
    nodes_all = row_len * row_n
    per_chunk = node_dev // tile_len
    row_ids = tile_rows[0, 0]
    col_ids = tile_cols[0, 0]
    chunk = row_ids // per_chunk
    high_i = chunk // (mid_n * core_n)
    mid_i = (chunk // core_n) % mid_n
    core_i = chunk % core_n
    placed = (core_i * mid_n * high_n + mid_i * high_n + high_i) * per_chunk + row_ids % per_chunk
    kept = (core_i == lax.axis_index("core")).astype(jnp.int32)
    fwd_placed = (kept * mid_n * high_n + mid_i * high_n + high_i) * per_chunk + row_ids % per_chunk
    weights_all = tile_weights[0, 0]
    live = tile_count[0, 0].reshape(1)
    source = doubling_gather(features, "row", row_n)
    source_tiles = source.reshape(col_tiles, tile_len, width)
    summed = slot_pass(live, fwd_placed, col_ids, weights_all, source_tiles, row_tiles, scale, False)
    partial_value = summed.reshape(row_len, width)
    half = row_len // 2
    partial_value = partial_value[half:] + lax.ppermute(
        partial_value[:half], "core", [(0, 1), (1, 0)]
    )
    partial_value = lax.psum_scatter(partial_value, "mid", scatter_dimension=0, tiled=True)
    partial_value = pair_scatter(partial_value, "high")
    aggregate = partial_value.astype(jnp.bfloat16)
    hidden, grad_own = dense_layer(aggregate, weight, cotangent)
    weight_part = lax.dot_general(
        aggregate, grad_own, (((0,), (0,)), ((), ())), preferred_element_type=jnp.float32
    )
    grad_agg = jnp.dot(grad_own, weight.T, preferred_element_type=jnp.float32).astype(jnp.bfloat16)
    every = ("row",) + col_axes
    levels = list(range((row_n * col_n).bit_length() - 1))
    weight_sum = butterfly_sum(
        weight_part, every, row_n * col_n, levels, ((core_n - 1).bit_length(), mid_n)
    )
    grad_source = pair_gather(grad_agg, "high")
    grad_source = lax.all_gather(grad_source, "mid", axis=0, tiled=True)
    grad_other = lax.ppermute(grad_source, "core", [(0, 1), (1, 0)])
    half_tiles = row_tiles // core_n
    own_tiles = grad_source.reshape(half_tiles, tile_len, width)
    other_tiles = grad_other.reshape(half_tiles, tile_len, width)
    halves = (core_i != lax.axis_index("core")).astype(jnp.int32)
    back_summed = back_pass(
        live, placed % half_tiles, col_ids, halves, weights_all, own_tiles, other_tiles,
        col_tiles, scale,
    )
    back_partial = back_summed.reshape(col_len, width)
    feature_grad = lax.psum_scatter(back_partial, "row", scatter_dimension=0, tiled=True).astype(
        jnp.bfloat16
    )
    weight_grad = weight_sum / math.sqrt(nodes_all)
    return (hidden, weight_grad, feature_grad)


def solution(mesh):
    row_n, col_n = mesh.shape["row"], mesh.shape["col"]
    core_n = 2
    high_n = 2
    mid_n = col_n // (high_n * core_n)
    sizes = (row_n, high_n, mid_n, core_n)
    fine = Mesh(mesh.devices.reshape(sizes), ("row", "high", "mid", "core"))
    col = ("high", "mid", "core")
    in_specs = (
        P(col + ("row",), None),
        P(),
        P(("row",) + col, None),
        P("row", col, None),
        P("row", col, None),
        P("row", col, None, None, None),
        P("row", col),
    )
    out_specs = (P(("row",) + col, None), P(), P(col + ("row",), None))
    return jax.shard_map(
        functools.partial(on_device, sizes=sizes),
        mesh=fine,
        in_specs=in_specs,
        out_specs=out_specs,
        check_vma=False,
    )
```

```python
import functools
import math

import jax
import jax.numpy as jnp
from jax import lax
from jax.experimental import pallas as pl
from jax.experimental.pallas import tpu as pltpu
from jax.sharding import Mesh
from jax.sharding import PartitionSpec as P

SPARSITY = 128


def slot_kernel(live_ref, rows_ref, cols_ref, tiles_ref, src_ref, out_ref, *, per_block, scale, transpose):
    block_id = pl.program_id(0)

    @pl.when(block_id == 0)
    def _():
        out_ref[...] = jnp.zeros_like(out_ref)

    live = live_ref[0]
    for k in range(per_block):
        slot = block_id * per_block + k

        @pl.when(slot < live)
        def _():
            tile_vals = tiles_ref[k].astype(jnp.bfloat16)
            if transpose:
                piece = src_ref[rows_ref[slot]]
                product = lax.dot_general(
                    tile_vals, piece, (((0,), (0,)), ((), ())), preferred_element_type=jnp.float32
                )
                target = cols_ref[slot]
            else:
                piece = src_ref[cols_ref[slot]]
                product = jnp.dot(tile_vals, piece, preferred_element_type=jnp.float32)
                target = rows_ref[slot]
            out_ref[target] += product

    @pl.when(block_id == pl.num_programs(0) - 1)
    def _():
        out_ref[...] = out_ref[...] * scale


def back_kernel(
    live_ref, rows_ref, cols_ref, halves_ref, tiles_ref, own_ref, other_ref, out_ref, *,
    per_block, scale
):
    block_id = pl.program_id(0)

    @pl.when(block_id == 0)
    def _():
        out_ref[...] = jnp.zeros_like(out_ref)

    live = live_ref[0]
    for k in range(per_block):
        slot = block_id * per_block + k
        for half, half_ref in ((0, own_ref), (1, other_ref)):

            @pl.when((slot < live) & (halves_ref[slot] == half))
            def _(half_ref=half_ref):
                tile_vals = tiles_ref[k].astype(jnp.bfloat16)
                piece = half_ref[rows_ref[slot]]
                product = lax.dot_general(
                    tile_vals, piece, (((0,), (0,)), ((), ())), preferred_element_type=jnp.float32
                )
                out_ref[cols_ref[slot]] += product

    @pl.when(block_id == pl.num_programs(0) - 1)
    def _():
        out_ref[...] = out_ref[...] * scale


def slot_pass(live, row_ids, col_ids, tiles, source_tiles, out_tiles, scale, transpose):
    slot_total, tile_len, _ = tiles.shape
    width = source_tiles.shape[-1]
    per_block = math.gcd(slot_total, 16)

    def tile_block(block_id, live_ref, rows_ref, cols_ref):
        last = jnp.maximum(live_ref[0] - 1, 0) // per_block
        return (jnp.minimum(block_id, last), 0, 0)

    def whole(block_id, live_ref, rows_ref, cols_ref):
        return (0, 0, 0)

    grid_spec = pltpu.PrefetchScalarGridSpec(
        num_scalar_prefetch=3,
        grid=(slot_total // per_block,),
        in_specs=[
            pl.BlockSpec((per_block, tile_len, tile_len), tile_block),
            pl.BlockSpec(source_tiles.shape, whole),
        ],
        out_specs=pl.BlockSpec((out_tiles, tile_len, width), whole),
    )
    return pl.pallas_call(
        functools.partial(slot_kernel, per_block=per_block, scale=scale, transpose=transpose),
        grid_spec=grid_spec,
        out_shape=jax.ShapeDtypeStruct((out_tiles, tile_len, width), jnp.float32),
        compiler_params=pltpu.CompilerParams(
            dimension_semantics=("arbitrary",), vmem_limit_bytes=48 * 1024 * 1024
        ),
    )(live, row_ids, col_ids, tiles, source_tiles)


def back_pass(live, row_ids, col_ids, halves, tiles, own_tiles, other_tiles, out_tiles, scale):
    slot_total, tile_len, _ = tiles.shape
    width = own_tiles.shape[-1]
    per_block = math.gcd(slot_total, 16)

    def tile_block(block_id, live_ref, rows_ref, cols_ref, halves_ref):
        last = jnp.maximum(live_ref[0] - 1, 0) // per_block
        return (jnp.minimum(block_id, last), 0, 0)

    def whole(block_id, live_ref, rows_ref, cols_ref, halves_ref):
        return (0, 0, 0)

    grid_spec = pltpu.PrefetchScalarGridSpec(
        num_scalar_prefetch=4,
        grid=(slot_total // per_block,),
        in_specs=[
            pl.BlockSpec((per_block, tile_len, tile_len), tile_block),
            pl.BlockSpec(own_tiles.shape, whole),
            pl.BlockSpec(other_tiles.shape, whole),
        ],
        out_specs=pl.BlockSpec((out_tiles, tile_len, width), whole),
    )
    return pl.pallas_call(
        functools.partial(back_kernel, per_block=per_block, scale=scale),
        grid_spec=grid_spec,
        out_shape=jax.ShapeDtypeStruct((out_tiles, tile_len, width), jnp.float32),
        compiler_params=pltpu.CompilerParams(
            dimension_semantics=("arbitrary",), vmem_limit_bytes=48 * 1024 * 1024
        ),
    )(live, row_ids, col_ids, halves, tiles, own_tiles, other_tiles)


def dense_layer(aggregate, weight, cotangent):
    preact = jnp.dot(aggregate, weight, preferred_element_type=jnp.float32)
    hidden = jax.nn.silu(preact).astype(jnp.bfloat16)
    sigma = jax.nn.sigmoid(preact)
    grad_pre = (cotangent.astype(jnp.float32) * sigma * (1.0 + preact * (1.0 - sigma))).astype(
        jnp.bfloat16
    )
    return (hidden, grad_pre)


def butterfly_sum(value, axes, count, levels, rings):
    def partner(i, level):
        for low_bit, ring_n in rings:
            if low_bit <= level < low_bit + ring_n.bit_length() - 1:
                label = [p ^ (p >> 1) for p in range(ring_n)]
                p = (i >> low_bit) % ring_n
                q = label.index(label[p] ^ (1 << (level - low_bit)))
                return i + ((q - p) << low_bit)
        return i ^ (1 << level)

    for level in levels:
        pairs = [(i, partner(i, level)) for i in range(count)]
        value = value + lax.ppermute(value, axes, pairs)
    return value


def doubling_gather(value, axis, count):
    own = lax.axis_index(axis)
    for level in range(count.bit_length() - 1):
        pairs = [(i, i ^ (1 << level)) for i in range(count)]
        other = lax.ppermute(value, axis, pairs)
        low = ((own >> level) & 1) == 0
        value = jnp.concatenate(
            [jnp.where(low, value, other), jnp.where(low, other, value)], axis=0
        )
    return value


def pair_scatter(value, axis):
    half = value.shape[0] // 2
    own = lax.axis_index(axis)
    keep = lax.dynamic_slice_in_dim(value, own * half, half, 0)
    send = lax.dynamic_slice_in_dim(value, (1 - own) * half, half, 0)
    return keep + lax.ppermute(send, axis, [(0, 1), (1, 0)])


def pair_gather(value, axis):
    own = lax.axis_index(axis)
    other = lax.ppermute(value, axis, [(0, 1), (1, 0)])
    first = jnp.where(own == 0, value, other)
    second = jnp.where(own == 0, other, value)
    return jnp.concatenate([first, second], axis=0)


def on_device(
    features, weight, cotangent, tile_rows, tile_cols, tile_weights, tile_count, *, sizes
):
    row_n, high_n, mid_n, core_n = sizes
    col_axes = ("high", "mid", "core")
    col_n = high_n * mid_n * core_n
    node_dev = cotangent.shape[0]
    width = features.shape[1]
    slot_total = tile_weights.shape[2]
    tile_len = tile_weights.shape[-1]
    sparsity_value = SPARSITY
    fan_value = slot_total * tile_len * tile_len // (node_dev * sparsity_value)
    scale = 1.0 / math.sqrt(2.0 * fan_value)
    row_len = node_dev * col_n
    col_len = node_dev * row_n
    row_tiles = row_len // tile_len
    col_tiles = col_len // tile_len
    nodes_all = row_len * row_n
    per_chunk = node_dev // tile_len
    row_ids = tile_rows[0, 0]
    col_ids = tile_cols[0, 0]
    chunk = row_ids // per_chunk
    high_i = chunk // (mid_n * core_n)
    mid_i = (chunk // core_n) % mid_n
    core_i = chunk % core_n
    placed = (core_i * mid_n * high_n + mid_i * high_n + high_i) * per_chunk + row_ids % per_chunk
    kept = (core_i == lax.axis_index("core")).astype(jnp.int32)
    fwd_placed = (kept * mid_n * high_n + mid_i * high_n + high_i) * per_chunk + row_ids % per_chunk
    weights_all = tile_weights[0, 0]
    live = tile_count[0, 0].reshape(1)
    source = doubling_gather(features, "row", row_n)
    source_tiles = source.reshape(col_tiles, tile_len, width)
    summed = slot_pass(live, fwd_placed, col_ids, weights_all, source_tiles, row_tiles, scale, False)
    partial_value = summed.reshape(row_len, width)
    half = row_len // 2
    partial_value = partial_value[half:] + lax.ppermute(
        partial_value[:half], "core", [(0, 1), (1, 0)]
    )
    partial_value = lax.psum_scatter(partial_value, "mid", scatter_dimension=0, tiled=True)
    partial_value = pair_scatter(partial_value, "high")
    aggregate = partial_value.astype(jnp.bfloat16)
    hidden, grad_own = dense_layer(aggregate, weight, cotangent)
    weight_part = lax.dot_general(
        aggregate, grad_own, (((0,), (0,)), ((), ())), preferred_element_type=jnp.float32
    )
    grad_agg = jnp.dot(grad_own, weight.T, preferred_element_type=jnp.float32).astype(jnp.bfloat16)
    every = ("row",) + col_axes
    levels = list(range((row_n * col_n).bit_length() - 1))
    mid_low = (core_n - 1).bit_length()
    x_n = 4 if row_n % 4 == 0 else row_n
    rings = ((mid_low, mid_n), ((col_n - 1).bit_length(), x_n))
    weight_sum = butterfly_sum(weight_part, every, row_n * col_n, levels, rings)
    grad_source = pair_gather(grad_agg, "high")
    grad_source = lax.all_gather(grad_source, "mid", axis=0, tiled=True)
    grad_other = lax.ppermute(grad_source, "core", [(0, 1), (1, 0)])
    half_tiles = row_tiles // core_n
    own_tiles = grad_source.reshape(half_tiles, tile_len, width)
    other_tiles = grad_other.reshape(half_tiles, tile_len, width)
    halves = (core_i != lax.axis_index("core")).astype(jnp.int32)
    back_summed = back_pass(
        live, placed % half_tiles, col_ids, halves, weights_all, own_tiles, other_tiles,
        col_tiles, scale,
    )
    back_partial = back_summed.reshape(col_len, width)
    feature_grad = lax.psum_scatter(back_partial, "row", scatter_dimension=0, tiled=True).astype(
        jnp.bfloat16
    )
    weight_grad = weight_sum / math.sqrt(nodes_all)
    return (hidden, weight_grad, feature_grad)


def solution(mesh):
    row_n, col_n = mesh.shape["row"], mesh.shape["col"]
    core_n = 2
    high_n = 2
    mid_n = col_n // (high_n * core_n)
    sizes = (row_n, high_n, mid_n, core_n)
    fine = Mesh(mesh.devices.reshape(sizes), ("row", "high", "mid", "core"))
    col = ("high", "mid", "core")
    in_specs = (
        P(col + ("row",), None),
        P(),
        P(("row",) + col, None),
        P("row", col, None),
        P("row", col, None),
        P("row", col, None, None, None),
        P("row", col),
    )
    out_specs = (P(("row",) + col, None), P(), P(col + ("row",), None))
    return jax.shard_map(
        functools.partial(on_device, sizes=sizes),
        mesh=fine,
        in_specs=in_specs,
        out_specs=out_specs,
        check_vma=False,
    )
```

```python
import functools
import math

import jax
import jax.numpy as jnp
from jax import lax
from jax.experimental import pallas as pl
from jax.experimental.pallas import tpu as pltpu
from jax.sharding import Mesh
from jax.sharding import PartitionSpec as P

SPARSITY = 128


def slot_kernel(live_ref, rows_ref, cols_ref, tiles_ref, src_ref, out_ref, *, per_block, scale, transpose):
    block_id = pl.program_id(0)

    @pl.when(block_id == 0)
    def _():
        out_ref[...] = jnp.zeros_like(out_ref)

    live = live_ref[0]
    for k in range(per_block):
        slot = block_id * per_block + k

        @pl.when(slot < live)
        def _():
            tile_vals = tiles_ref[k].astype(jnp.bfloat16)
            if transpose:
                piece = src_ref[rows_ref[slot]]
                product = lax.dot_general(
                    tile_vals, piece, (((0,), (0,)), ((), ())), preferred_element_type=jnp.float32
                )
                target = cols_ref[slot]
            else:
                piece = src_ref[cols_ref[slot]]
                product = jnp.dot(tile_vals, piece, preferred_element_type=jnp.float32)
                target = rows_ref[slot]
            out_ref[target] += product

    @pl.when(block_id == pl.num_programs(0) - 1)
    def _():
        out_ref[...] = out_ref[...] * scale


def back_kernel(
    live_ref, rows_ref, cols_ref, halves_ref, tiles_ref, own_ref, other_ref, out_ref, *,
    per_block, scale
):
    block_id = pl.program_id(0)

    @pl.when(block_id == 0)
    def _():
        out_ref[...] = jnp.zeros_like(out_ref)

    live = live_ref[0]
    for k in range(per_block):
        slot = block_id * per_block + k
        for half, half_ref in ((0, own_ref), (1, other_ref)):

            @pl.when((slot < live) & (halves_ref[slot] == half))
            def _(half_ref=half_ref):
                tile_vals = tiles_ref[k].astype(jnp.bfloat16)
                piece = half_ref[rows_ref[slot]]
                product = lax.dot_general(
                    tile_vals, piece, (((0,), (0,)), ((), ())), preferred_element_type=jnp.float32
                )
                out_ref[cols_ref[slot]] += product

    @pl.when(block_id == pl.num_programs(0) - 1)
    def _():
        out_ref[...] = out_ref[...] * scale


def slot_pass(live, row_ids, col_ids, tiles, source_tiles, out_tiles, scale, transpose):
    slot_total, tile_len, _ = tiles.shape
    width = source_tiles.shape[-1]
    per_block = math.gcd(slot_total, 16)

    def tile_block(block_id, live_ref, rows_ref, cols_ref):
        last = jnp.maximum(live_ref[0] - 1, 0) // per_block
        return (jnp.minimum(block_id, last), 0, 0)

    def whole(block_id, live_ref, rows_ref, cols_ref):
        return (0, 0, 0)

    grid_spec = pltpu.PrefetchScalarGridSpec(
        num_scalar_prefetch=3,
        grid=(slot_total // per_block,),
        in_specs=[
            pl.BlockSpec((per_block, tile_len, tile_len), tile_block),
            pl.BlockSpec(source_tiles.shape, whole),
        ],
        out_specs=pl.BlockSpec((out_tiles, tile_len, width), whole),
    )
    return pl.pallas_call(
        functools.partial(slot_kernel, per_block=per_block, scale=scale, transpose=transpose),
        grid_spec=grid_spec,
        out_shape=jax.ShapeDtypeStruct((out_tiles, tile_len, width), jnp.float32),
        compiler_params=pltpu.CompilerParams(
            dimension_semantics=("arbitrary",), vmem_limit_bytes=48 * 1024 * 1024
        ),
    )(live, row_ids, col_ids, tiles, source_tiles)


def back_pass(live, row_ids, col_ids, halves, tiles, own_tiles, other_tiles, out_tiles, scale):
    slot_total, tile_len, _ = tiles.shape
    width = own_tiles.shape[-1]
    per_block = math.gcd(slot_total, 16)

    def tile_block(block_id, live_ref, rows_ref, cols_ref, halves_ref):
        last = jnp.maximum(live_ref[0] - 1, 0) // per_block
        return (jnp.minimum(block_id, last), 0, 0)

    def whole(block_id, live_ref, rows_ref, cols_ref, halves_ref):
        return (0, 0, 0)

    grid_spec = pltpu.PrefetchScalarGridSpec(
        num_scalar_prefetch=4,
        grid=(slot_total // per_block,),
        in_specs=[
            pl.BlockSpec((per_block, tile_len, tile_len), tile_block),
            pl.BlockSpec(own_tiles.shape, whole),
            pl.BlockSpec(other_tiles.shape, whole),
        ],
        out_specs=pl.BlockSpec((out_tiles, tile_len, width), whole),
    )
    return pl.pallas_call(
        functools.partial(back_kernel, per_block=per_block, scale=scale),
        grid_spec=grid_spec,
        out_shape=jax.ShapeDtypeStruct((out_tiles, tile_len, width), jnp.float32),
        compiler_params=pltpu.CompilerParams(
            dimension_semantics=("arbitrary",), vmem_limit_bytes=48 * 1024 * 1024
        ),
    )(live, row_ids, col_ids, halves, tiles, own_tiles, other_tiles)


def dense_layer(aggregate, weight, cotangent):
    preact = jnp.dot(aggregate, weight, preferred_element_type=jnp.float32)
    hidden = jax.nn.silu(preact).astype(jnp.bfloat16)
    sigma = jax.nn.sigmoid(preact)
    grad_pre = (cotangent.astype(jnp.float32) * sigma * (1.0 + preact * (1.0 - sigma))).astype(
        jnp.bfloat16
    )
    return (hidden, grad_pre)


def butterfly_sum(value, axes, count, levels, ring_bits):
    low_bit, ring_n = ring_bits
    label = [p ^ (p >> 1) for p in range(ring_n)]
    position = {g: p for p, g in enumerate(label)}

    def partner(i, level):
        if low_bit <= level < low_bit + ring_n.bit_length() - 1:
            p = (i >> low_bit) % ring_n
            q = position[label[p] ^ (1 << (level - low_bit))]
            return i + ((q - p) << low_bit)
        return i ^ (1 << level)

    for level in levels:
        pairs = [(i, partner(i, level)) for i in range(count)]
        value = value + lax.ppermute(value, axes, pairs)
    return value


def doubling_gather(value, axis, count):
    own = lax.axis_index(axis)
    for level in range(count.bit_length() - 1):
        pairs = [(i, i ^ (1 << level)) for i in range(count)]
        other = lax.ppermute(value, axis, pairs)
        low = ((own >> level) & 1) == 0
        value = jnp.concatenate(
            [jnp.where(low, value, other), jnp.where(low, other, value)], axis=0
        )
    return value


def pair_scatter(value, axis):
    half = value.shape[0] // 2
    own = lax.axis_index(axis)
    keep = lax.dynamic_slice_in_dim(value, own * half, half, 0)
    send = lax.dynamic_slice_in_dim(value, (1 - own) * half, half, 0)
    return keep + lax.ppermute(send, axis, [(0, 1), (1, 0)])


def pair_gather(value, axis):
    own = lax.axis_index(axis)
    other = lax.ppermute(value, axis, [(0, 1), (1, 0)])
    first = jnp.where(own == 0, value, other)
    second = jnp.where(own == 0, other, value)
    return jnp.concatenate([first, second], axis=0)


def on_device(
    features, weight, cotangent, tile_rows, tile_cols, tile_weights, tile_count, *, sizes
):
    row_n, high_n, mid_n, core_n = sizes
    col_axes = ("high", "mid", "core")
    col_n = high_n * mid_n * core_n
    node_dev = cotangent.shape[0]
    width = features.shape[1]
    slot_total = tile_weights.shape[2]
    tile_len = tile_weights.shape[-1]
    sparsity_value = SPARSITY
    fan_value = slot_total * tile_len * tile_len // (node_dev * sparsity_value)
    scale = 1.0 / math.sqrt(2.0 * fan_value)
    row_len = node_dev * col_n
    col_len = node_dev * row_n
    row_tiles = row_len // tile_len
    col_tiles = col_len // tile_len
    nodes_all = row_len * row_n
    per_chunk = node_dev // tile_len
    row_ids = tile_rows[0, 0]
    col_ids = tile_cols[0, 0]
    chunk = row_ids // per_chunk
    high_i = chunk // (mid_n * core_n)
    mid_i = (chunk // core_n) % mid_n
    core_i = chunk % core_n
    placed = (core_i * mid_n * high_n + mid_i * high_n + high_i) * per_chunk + row_ids % per_chunk
    kept = (core_i == lax.axis_index("core")).astype(jnp.int32)
    fwd_placed = (kept * mid_n * high_n + mid_i * high_n + high_i) * per_chunk + row_ids % per_chunk
    weights_all = tile_weights[0, 0]
    live = tile_count[0, 0].reshape(1)
    source = doubling_gather(features, "row", row_n)
    source_tiles = source.reshape(col_tiles, tile_len, width)
    summed = slot_pass(live, fwd_placed, col_ids, weights_all, source_tiles, row_tiles, scale, False)
    partial_value = summed.reshape(row_len, width)
    half = row_len // 2
    partial_value = partial_value[half:] + lax.ppermute(
        partial_value[:half], "core", [(0, 1), (1, 0)]
    )
    partial_value = lax.psum_scatter(partial_value, "mid", scatter_dimension=0, tiled=True)
    partial_value = pair_scatter(partial_value, "high")
    aggregate = partial_value.astype(jnp.bfloat16)
    hidden, grad_own = dense_layer(aggregate, weight, cotangent)
    weight_part = lax.dot_general(
        aggregate, grad_own, (((0,), (0,)), ((), ())), preferred_element_type=jnp.float32
    )
    grad_agg = jnp.dot(grad_own, weight.T, preferred_element_type=jnp.float32).astype(jnp.bfloat16)
    every = ("row",) + col_axes
    high_level = (core_n * mid_n - 1).bit_length()
    levels = [level for level in range((row_n * col_n).bit_length() - 1) if level != high_level]
    levels = levels + [high_level]
    weight_sum = butterfly_sum(
        weight_part, every, row_n * col_n, levels, ((core_n - 1).bit_length(), mid_n)
    )
    grad_source = pair_gather(grad_agg, "high")
    grad_source = lax.all_gather(grad_source, "mid", axis=0, tiled=True)
    grad_other = lax.ppermute(grad_source, "core", [(0, 1), (1, 0)])
    half_tiles = row_tiles // core_n
    own_tiles = grad_source.reshape(half_tiles, tile_len, width)
    other_tiles = grad_other.reshape(half_tiles, tile_len, width)
    halves = (core_i != lax.axis_index("core")).astype(jnp.int32)
    back_summed = back_pass(
        live, placed % half_tiles, col_ids, halves, weights_all, own_tiles, other_tiles,
        col_tiles, scale,
    )
    back_partial = back_summed.reshape(col_len, width)
    feature_grad = lax.psum_scatter(back_partial, "row", scatter_dimension=0, tiled=True).astype(
        jnp.bfloat16
    )
    weight_grad = weight_sum / math.sqrt(nodes_all)
    return (hidden, weight_grad, feature_grad)


def solution(mesh):
    row_n, col_n = mesh.shape["row"], mesh.shape["col"]
    core_n = 2
    high_n = 2
    mid_n = col_n // (high_n * core_n)
    sizes = (row_n, high_n, mid_n, core_n)
    fine = Mesh(mesh.devices.reshape(sizes), ("row", "high", "mid", "core"))
    col = ("high", "mid", "core")
    in_specs = (
        P(col + ("row",), None),
        P(),
        P(("row",) + col, None),
        P("row", col, None),
        P("row", col, None),
        P("row", col, None, None, None),
        P("row", col),
    )
    out_specs = (P(("row",) + col, None), P(), P(col + ("row",), None))
    return jax.shard_map(
        functools.partial(on_device, sizes=sizes),
        mesh=fine,
        in_specs=in_specs,
        out_specs=out_specs,
        check_vma=False,
    )
```

```python
import functools
import math

import jax
import jax.numpy as jnp
from jax import lax
from jax.experimental import pallas as pl
from jax.experimental.pallas import tpu as pltpu
from jax.sharding import Mesh
from jax.sharding import PartitionSpec as P

SPARSITY = 128


def slot_kernel(live_ref, rows_ref, cols_ref, tiles_ref, src_ref, out_ref, *, per_block, scale, transpose):
    block_id = pl.program_id(0)

    @pl.when(block_id == 0)
    def _():
        out_ref[...] = jnp.zeros_like(out_ref)

    live = live_ref[0]
    for k in range(per_block):
        slot = block_id * per_block + k

        @pl.when(slot < live)
        def _():
            tile_vals = tiles_ref[k].astype(jnp.bfloat16)
            if transpose:
                piece = src_ref[rows_ref[slot]]
                product = lax.dot_general(
                    tile_vals, piece, (((0,), (0,)), ((), ())), preferred_element_type=jnp.float32
                )
                target = cols_ref[slot]
            else:
                piece = src_ref[cols_ref[slot]]
                product = jnp.dot(tile_vals, piece, preferred_element_type=jnp.float32)
                target = rows_ref[slot]
            out_ref[target] += product

    @pl.when(block_id == pl.num_programs(0) - 1)
    def _():
        out_ref[...] = out_ref[...] * scale


def back_kernel(
    live_ref, rows_ref, cols_ref, halves_ref, tiles_ref, own_ref, other_ref, out_ref, *,
    per_block, scale
):
    block_id = pl.program_id(0)

    @pl.when(block_id == 0)
    def _():
        out_ref[...] = jnp.zeros_like(out_ref)

    live = live_ref[0]
    for k in range(per_block):
        slot = block_id * per_block + k
        for half, half_ref in ((0, own_ref), (1, other_ref)):

            @pl.when((slot < live) & (halves_ref[slot] == half))
            def _(half_ref=half_ref):
                tile_vals = tiles_ref[k].astype(jnp.bfloat16)
                piece = half_ref[rows_ref[slot]]
                product = lax.dot_general(
                    tile_vals, piece, (((0,), (0,)), ((), ())), preferred_element_type=jnp.float32
                )
                out_ref[cols_ref[slot]] += product

    @pl.when(block_id == pl.num_programs(0) - 1)
    def _():
        out_ref[...] = out_ref[...] * scale


def slot_pass(live, row_ids, col_ids, tiles, source_tiles, out_tiles, scale, transpose):
    slot_total, tile_len, _ = tiles.shape
    width = source_tiles.shape[-1]
    per_block = math.gcd(slot_total, 16)

    def tile_block(block_id, live_ref, rows_ref, cols_ref):
        last = jnp.maximum(live_ref[0] - 1, 0) // per_block
        return (jnp.minimum(block_id, last), 0, 0)

    def whole(block_id, live_ref, rows_ref, cols_ref):
        return (0, 0, 0)

    grid_spec = pltpu.PrefetchScalarGridSpec(
        num_scalar_prefetch=3,
        grid=(slot_total // per_block,),
        in_specs=[
            pl.BlockSpec((per_block, tile_len, tile_len), tile_block),
            pl.BlockSpec(source_tiles.shape, whole),
        ],
        out_specs=pl.BlockSpec((out_tiles, tile_len, width), whole),
    )
    return pl.pallas_call(
        functools.partial(slot_kernel, per_block=per_block, scale=scale, transpose=transpose),
        grid_spec=grid_spec,
        out_shape=jax.ShapeDtypeStruct((out_tiles, tile_len, width), jnp.float32),
        compiler_params=pltpu.CompilerParams(
            dimension_semantics=("arbitrary",), vmem_limit_bytes=48 * 1024 * 1024
        ),
    )(live, row_ids, col_ids, tiles, source_tiles)


def back_pass(live, row_ids, col_ids, halves, tiles, own_tiles, other_tiles, out_tiles, scale):
    slot_total, tile_len, _ = tiles.shape
    width = own_tiles.shape[-1]
    per_block = math.gcd(slot_total, 16)

    def tile_block(block_id, live_ref, rows_ref, cols_ref, halves_ref):
        last = jnp.maximum(live_ref[0] - 1, 0) // per_block
        return (jnp.minimum(block_id, last), 0, 0)

    def whole(block_id, live_ref, rows_ref, cols_ref, halves_ref):
        return (0, 0, 0)

    grid_spec = pltpu.PrefetchScalarGridSpec(
        num_scalar_prefetch=4,
        grid=(slot_total // per_block,),
        in_specs=[
            pl.BlockSpec((per_block, tile_len, tile_len), tile_block),
            pl.BlockSpec(own_tiles.shape, whole),
            pl.BlockSpec(other_tiles.shape, whole),
        ],
        out_specs=pl.BlockSpec((out_tiles, tile_len, width), whole),
    )
    return pl.pallas_call(
        functools.partial(back_kernel, per_block=per_block, scale=scale),
        grid_spec=grid_spec,
        out_shape=jax.ShapeDtypeStruct((out_tiles, tile_len, width), jnp.float32),
        compiler_params=pltpu.CompilerParams(
            dimension_semantics=("arbitrary",), vmem_limit_bytes=48 * 1024 * 1024
        ),
    )(live, row_ids, col_ids, halves, tiles, own_tiles, other_tiles)


def dense_layer(aggregate, weight, cotangent):
    preact = jnp.dot(aggregate, weight, preferred_element_type=jnp.float32)
    hidden = jax.nn.silu(preact).astype(jnp.bfloat16)
    sigma = jax.nn.sigmoid(preact)
    grad_pre = (cotangent.astype(jnp.float32) * sigma * (1.0 + preact * (1.0 - sigma))).astype(
        jnp.bfloat16
    )
    return (hidden, grad_pre)


def butterfly_sum(value, axes, count, levels, ring_bits):
    low_bit, ring_n = ring_bits
    label = [p ^ (p >> 1) for p in range(ring_n)]
    position = {g: p for p, g in enumerate(label)}

    def partner(i, level):
        if low_bit <= level < low_bit + ring_n.bit_length() - 1:
            p = (i >> low_bit) % ring_n
            q = position[label[p] ^ (1 << (level - low_bit))]
            return i + ((q - p) << low_bit)
        return i ^ (1 << level)

    for level in levels:
        pairs = [(i, partner(i, level)) for i in range(count)]
        value = value + lax.ppermute(value, axes, pairs)
    return value


def doubling_gather(value, axis, count):
    own = lax.axis_index(axis)
    for level in range(count.bit_length() - 1):
        pairs = [(i, i ^ (1 << level)) for i in range(count)]
        other = lax.ppermute(value, axis, pairs)
        low = ((own >> level) & 1) == 0
        value = jnp.concatenate(
            [jnp.where(low, value, other), jnp.where(low, other, value)], axis=0
        )
    return value


def pair_scatter(value, axis):
    half = value.shape[0] // 2
    own = lax.axis_index(axis)
    keep = lax.dynamic_slice_in_dim(value, own * half, half, 0)
    send = lax.dynamic_slice_in_dim(value, (1 - own) * half, half, 0)
    return keep + lax.ppermute(send, axis, [(0, 1), (1, 0)])


def pair_gather(value, axis):
    own = lax.axis_index(axis)
    other = lax.ppermute(value, axis, [(0, 1), (1, 0)])
    first = jnp.where(own == 0, value, other)
    second = jnp.where(own == 0, other, value)
    return jnp.concatenate([first, second], axis=0)


def on_device(
    features, weight, cotangent, tile_rows, tile_cols, tile_weights, tile_count, *, sizes
):
    row_n, high_n, mid_n, core_n = sizes
    col_axes = ("high", "mid", "core")
    col_n = high_n * mid_n * core_n
    node_dev = cotangent.shape[0]
    width = features.shape[1]
    slot_total = tile_weights.shape[2]
    tile_len = tile_weights.shape[-1]
    sparsity_value = SPARSITY
    fan_value = slot_total * tile_len * tile_len // (node_dev * sparsity_value)
    scale = 1.0 / math.sqrt(2.0 * fan_value)
    row_len = node_dev * col_n
    col_len = node_dev * row_n
    row_tiles = row_len // tile_len
    col_tiles = col_len // tile_len
    nodes_all = row_len * row_n
    per_chunk = node_dev // tile_len
    row_ids = tile_rows[0, 0]
    col_ids = tile_cols[0, 0]
    chunk = row_ids // per_chunk
    high_i = chunk // (mid_n * core_n)
    mid_i = (chunk // core_n) % mid_n
    core_i = chunk % core_n
    placed = (core_i * mid_n * high_n + mid_i * high_n + high_i) * per_chunk + row_ids % per_chunk
    kept = (core_i == lax.axis_index("core")).astype(jnp.int32)
    high_kept = (high_i == lax.axis_index("high")).astype(jnp.int32)
    fwd_placed = (kept * mid_n * high_n + mid_i * high_n + high_kept) * per_chunk
    fwd_placed = fwd_placed + row_ids % per_chunk
    weights_all = tile_weights[0, 0]
    live = tile_count[0, 0].reshape(1)
    source = doubling_gather(features, "row", row_n)
    source_tiles = source.reshape(col_tiles, tile_len, width)
    summed = slot_pass(live, fwd_placed, col_ids, weights_all, source_tiles, row_tiles, scale, False)
    partial_value = summed.reshape(row_len, width)
    half = row_len // 2
    partial_value = partial_value[half:] + lax.ppermute(
        partial_value[:half], "core", [(0, 1), (1, 0)]
    )
    partial_value = lax.psum_scatter(partial_value, "mid", scatter_dimension=0, tiled=True)
    half = partial_value.shape[0] // 2
    partial_value = partial_value[half:] + lax.ppermute(
        partial_value[:half], "high", [(0, 1), (1, 0)]
    )
    aggregate = partial_value.astype(jnp.bfloat16)
    hidden, grad_own = dense_layer(aggregate, weight, cotangent)
    weight_part = lax.dot_general(
        aggregate, grad_own, (((0,), (0,)), ((), ())), preferred_element_type=jnp.float32
    )
    grad_agg = jnp.dot(grad_own, weight.T, preferred_element_type=jnp.float32).astype(jnp.bfloat16)
    every = ("row",) + col_axes
    high_level = (core_n * mid_n - 1).bit_length()
    levels = [level for level in range((row_n * col_n).bit_length() - 1) if level != high_level]
    levels = levels + [high_level]
    weight_sum = butterfly_sum(
        weight_part, every, row_n * col_n, levels, ((core_n - 1).bit_length(), mid_n)
    )
    grad_source = pair_gather(grad_agg, "high")
    grad_source = lax.all_gather(grad_source, "mid", axis=0, tiled=True)
    grad_other = lax.ppermute(grad_source, "core", [(0, 1), (1, 0)])
    half_tiles = row_tiles // core_n
    own_tiles = grad_source.reshape(half_tiles, tile_len, width)
    other_tiles = grad_other.reshape(half_tiles, tile_len, width)
    halves = (core_i != lax.axis_index("core")).astype(jnp.int32)
    back_summed = back_pass(
        live, placed % half_tiles, col_ids, halves, weights_all, own_tiles, other_tiles,
        col_tiles, scale,
    )
    back_partial = back_summed.reshape(col_len, width)
    feature_grad = lax.psum_scatter(back_partial, "row", scatter_dimension=0, tiled=True).astype(
        jnp.bfloat16
    )
    weight_grad = weight_sum / math.sqrt(nodes_all)
    return (hidden, weight_grad, feature_grad)


def solution(mesh):
    row_n, col_n = mesh.shape["row"], mesh.shape["col"]
    core_n = 2
    high_n = 2
    mid_n = col_n // (high_n * core_n)
    sizes = (row_n, high_n, mid_n, core_n)
    fine = Mesh(mesh.devices.reshape(sizes), ("row", "high", "mid", "core"))
    col = ("high", "mid", "core")
    in_specs = (
        P(col + ("row",), None),
        P(),
        P(("row",) + col, None),
        P("row", col, None),
        P("row", col, None),
        P("row", col, None, None, None),
        P("row", col),
    )
    out_specs = (P(("row",) + col, None), P(), P(col + ("row",), None))
    return jax.shard_map(
        functools.partial(on_device, sizes=sizes),
        mesh=fine,
        in_specs=in_specs,
        out_specs=out_specs,
        check_vma=False,
    )
```
